1024 devices in a mesh: ctx: 64 (over x, y), head: 16 (over z, core).
Axes of the slice: x: 8, y: 8, z: 8, core: 2. Of those that a mesh axis runs over, the one named last changes fastest.
Arguments:
- queries: bfloat16 [8192, 4096], P(('ctx', 'head')), may hold values from -6 to 6
- keys: bfloat16 [8192, 4096], P(('ctx', 'head')), may hold values from -6 to 6
- values: bfloat16 [8192, 8192], P(('ctx', 'head')), may hold values from -6 to 6
- grad_out: bfloat16 [8192, 8192], P('ctx', 'head'), may hold values from -6 to 6
- log_decay: float32 [16, 8192], P('head', 'ctx'), may hold values from -1 to 0
- doc_lengths: int32 [32], replicated, may hold values from 1 to 2048, 8192 in all
Outputs:
- retained: bfloat16 [8192, 8192], P('ctx', 'head')
- query_gradient: bfloat16 [8192, 4096], P('ctx', 'head')
- grad_k: bfloat16 [8192, 4096], P('ctx', 'head')
- value_gradient: bfloat16 [8192, 8192], P('ctx', 'head')
The draws below stay inside these ranges and needn't reach their ends.
Inputs may be any that keep to these rules, and one draw needn't show every extreme that they name: `doc_lengths`: the 32 lengths sum to 8192; the largest is exactly 2048.
All inputs are finite; a program needn't handle non-finite values.
Results may differ from the reference program's by a relative error of at most 0.0056.
Values may be sent and summed in bfloat16 or wider, within the bound.
No kernel may reach another device: no remote copies, remote signals or barrier semaphores. Data moves between devices by JAX's collectives and lax.ppermute only.
A program may use at most 32 MiB of HBM per device.

```python
import math
import jax
import jax.numpy as jnp
import numpy as np
from jax import lax

DK = 256
DV = 512
BLOCK = 128
NDOCS = 32
TOK_DEV = 128
HEADS = 16
WINDOW_TOKENS = 8192
LONGEST = 2048


spike_total_count = 3


def draw_log_decay(key, part):
    key_sequence = jax.random.split(key, 7)
    order = jax.random.permutation(key_sequence[0], HEADS)
    fast_heads = order < max(HEADS // 2, 1)
    fast_rate = jnp.exp(jax.random.uniform(key_sequence[1], (HEADS,), jnp.float32, math.log(1.0 / 50.0), math.log(1.0 / 30.0)))
    slow_rate = jnp.exp(jax.random.uniform(key_sequence[2], (HEADS,), jnp.float32, math.log(0.05), math.log(0.3))) / WINDOW_TOKENS
    baseline_decay_rate = jnp.where(fast_heads, fast_rate, slow_rate)
    shard_count = WINDOW_TOKENS // TOK_DEV
    partition_gain = jnp.exp(jax.random.uniform(key_sequence[3], (HEADS, shard_count), jnp.float32, math.log(0.5), math.log(2.0)))
    partition_gain = jnp.repeat(partition_gain, TOK_DEV, axis=1)
    jitter_amplitude = jnp.exp(jax.random.uniform(key_sequence[4], (HEADS, WINDOW_TOKENS), jnp.float32, math.log(0.6), math.log(1.3)))
    spike_locations = jax.random.randint(key_sequence[5], (spike_total_count,), 0, WINDOW_TOKENS)
    spike_removals = jax.random.uniform(key_sequence[6], (spike_total_count,), jnp.float32, math.log(0.5), math.log(0.8))
    spike_matches = (jnp.arange(WINDOW_TOKENS, dtype=jnp.int32)[:, None] == spike_locations[None, :]).astype(jnp.float32)
    spike_events = jnp.sum(spike_matches * spike_removals[None, :], axis=1)
    return -baseline_decay_rate[:, None] * partition_gain * jitter_amplitude + spike_events[None, :]


def shard_levels(own_key, shape, pieces, low, top_value):
    def one(position, blocks):
        steps = jax.random.uniform(jax.random.fold_in(jax.random.fold_in(own_key, 6), position), (blocks,), jnp.float32, low / len(pieces), top_value / len(pieces))
        return jnp.repeat(jnp.exp(steps), shape[position] // blocks).reshape((-1,) + (1,) * (len(shape) - position - 1))

    gain = one(*pieces[0])
    for cut in pieces[1:]:
        gain = gain * one(*cut)
    return gain


def length_profile(amount, total, most, skew):
    weights = [(1 << 20) // math.isqrt(rank ** skew) + 1 for rank in range(2, amount + 1)]
    surplus, counts = total - most - (amount - 1), [1] * (amount - 1)
    while surplus > 0:
        free = [i for i in range(amount - 1) if counts[i] < most]
        whole, budget = sum([weights[i] for i in free]), surplus
        for i in free:
            extra = min(most - counts[i], max(1, budget * weights[i] // whole), surplus)
            counts[i] = counts[i] + extra
            surplus = surplus - extra
    return np.array([most] + counts)


def uneven_parts(key, number_of, total, most, skew):
    if number_of == 2:
        one = jax.random.randint(key, (), max(1, total - most), min(most, total - 1) + 1)
        return jnp.stack([one, total - one])
    tallies = jnp.asarray(length_profile(number_of, total, most, skew), jnp.int32)
    couples = (number_of - 1) // 2
    source_of, taker = tallies[1:1 + 2 * couples:2], tallies[2:2 + 2 * couples:2]
    room = jnp.minimum(source_of - 1, most - taker)
    shifted = jax.random.randint(jax.random.fold_in(key, 1), (couples,), 0, 1 << 20) % (room + 1)
    tallies = tallies.at[1:1 + 2 * couples:2].set(source_of - shifted).at[2:2 + 2 * couples:2].set(taker + shifted)
    return tallies[jax.random.permutation(jax.random.fold_in(key, 2), number_of)]


def noise(key, shape, deviation, most, cuts=(), kind=jnp.bfloat16):
    drawn = deviation * jax.random.normal(key, shape, jnp.float32)
    if cuts:
        drawn = drawn * shard_levels(key, shape, cuts, -0.22, 0.18)
    return jnp.clip(drawn, -most, most).astype(kind)


def setup_inputs(seed: int = 0) -> dict:
    seeds = jax.random.split(jax.random.key(seed), 7)
    return {
        "queries": noise(seeds[0], (WINDOW_TOKENS, HEADS * DK), 1.0, 6.0, ((0, 1024),)),
        "keys": noise(seeds[1], (WINDOW_TOKENS, HEADS * DK), 1.0, 6.0, ((0, 1024),)),
        "values": noise(seeds[2], (WINDOW_TOKENS, HEADS * DV), 1.0, 6.0, ((0, 1024),)),
        "grad_out": noise(seeds[3], (WINDOW_TOKENS, HEADS * DV), 1.0, 6.0, ((0, 64), (1, 16))),
        "log_decay": draw_log_decay(jax.random.fold_in(seeds[6], 71), 0),
        "doc_lengths": uneven_parts(seeds[5], NDOCS, WINDOW_TOKENS, LONGEST, 2).astype(jnp.int32),
    }


def rounded(values):
    return lax.optimization_barrier(values.astype(jnp.bfloat16)).astype(jnp.float32)


def document_ids(doc_lengths, first_place, span_length):
    starts = jnp.cumsum(doc_lengths, dtype=jnp.int32) - doc_lengths
    places = first_place - 1 + jnp.arange(span_length + 1, dtype=jnp.int32)
    return jnp.sum((starts[None, :] <= places[:, None]).astype(jnp.int32), axis=1) - 1


def decay_tables(log_rates, doc_ids, block_size, score_scaling):
    block_count = log_rates.shape[0] // block_size
    cumulated = jnp.cumsum(log_rates.reshape(block_count, block_size), axis=1)
    before = doc_ids[0:block_count * block_size:block_size]
    own_ids = doc_ids[1:].reshape(block_count, block_size)
    carried = (own_ids == before[:, None]).astype(jnp.float32)
    last_ids = own_ids[:, block_size - 1]
    tail_mask = (own_ids == last_ids[:, None]).astype(jnp.float32)
    block_decay = jnp.exp(cumulated[:, block_size - 1]) * carried[:, block_size - 1]
    row_index = lax.broadcasted_iota(jnp.int32, (block_size, block_size), 0)
    column_index = lax.broadcasted_iota(jnp.int32, (block_size, block_size), 1)
    inside = (own_ids[:, :, None] == own_ids[:, None, :]) & (row_index >= column_index)[None]
    decay_gaps = cumulated[:, :, None] - cumulated[:, None, :]
    weights = jnp.where(inside, jnp.exp(jnp.where(inside, decay_gaps, 0.0)), 0.0) * score_scaling
    per_head_decay_rate = jnp.exp(cumulated) * carried
    tail_decay = jnp.exp(cumulated[:, block_size - 1:] - cumulated) * tail_mask
    return weights, per_head_decay_rate, tail_decay, block_decay


def forward_step(state, inputs):
    decay, update = inputs
    return decay * state + update, state


def reference(queries, keys, values, grad_out, log_decay, doc_lengths):
    doc_ids = document_ids(doc_lengths, 0, WINDOW_TOKENS)
    block_count = WINDOW_TOKENS // BLOCK
    score_scaling = (DK * BLOCK) ** -0.5

    def one_head(head):
        query_block_list = lax.dynamic_slice_in_dim(queries, head * DK, DK, 1).astype(jnp.float32).reshape(block_count, BLOCK, DK)
        key_blocks = lax.dynamic_slice_in_dim(keys, head * DK, DK, 1).astype(jnp.float32).reshape(block_count, BLOCK, DK)
        value_block_list = lax.dynamic_slice_in_dim(values, head * DV, DV, 1).astype(jnp.float32).reshape(block_count, BLOCK, DV)
        gradient_block_list = lax.dynamic_slice_in_dim(grad_out, head * DV, DV, 1).astype(jnp.float32).reshape(block_count, BLOCK, DV)
        log_rates = lax.dynamic_index_in_dim(log_decay, head, 0, keepdims=False)
        weights, per_head_decay_rate, tail_decay, block_decay = decay_tables(log_rates, doc_ids, BLOCK, score_scaling)
        zero_state = jnp.zeros((DK, DV), jnp.float32)
        keyed_blocks = rounded(key_blocks * tail_decay[:, :, None])
        updates = jnp.einsum('ncd,nce->nde', keyed_blocks, value_block_list)
        last_state, states = lax.scan(forward_step, zero_state, (block_decay, updates))
        queried = rounded(query_block_list * (per_head_decay_rate * score_scaling)[:, :, None])
        back_updates = jnp.einsum('ncd,nce->nde', queried, gradient_block_list)
        first_back, ends = lax.scan(forward_step, zero_state, (block_decay, back_updates), reverse=True)
        lowered_state = rounded(states)
        back_low = rounded(ends)
        scores = jnp.einsum('nid,njd->nij', query_block_list, key_blocks)
        attention_weights = rounded(scores * weights)
        retained = jnp.einsum('xho,xoy->xhy', query_block_list, lowered_state) * (per_head_decay_rate * score_scaling)[:, :, None]
        retained = retained + jnp.einsum('bcv,bvd->bcd', attention_weights, value_block_list)
        score_gradient = jnp.einsum('ysb,ytb->yst', gradient_block_list, value_block_list)
        gprobs = rounded(score_gradient * weights)
        query_gradient = jnp.einsum('srj,sqj->srq', gradient_block_list, lowered_state) * (per_head_decay_rate * score_scaling)[:, :, None]
        query_gradient = query_gradient + jnp.einsum('nij,njd->nid', gprobs, key_blocks)
        grad_k = jnp.einsum('nje,nde->njd', value_block_list, back_low) * tail_decay[:, :, None]
        grad_k = grad_k + jnp.einsum('nij,nid->njd', gprobs, query_block_list)
        value_gradient = jnp.einsum('njd,nde->nje', key_blocks, back_low) * tail_decay[:, :, None]
        value_gradient = value_gradient + jnp.einsum('glu,glx->gux', attention_weights, gradient_block_list)
        return (retained.reshape(WINDOW_TOKENS, DV).astype(jnp.bfloat16), query_gradient.reshape(WINDOW_TOKENS, DK).astype(jnp.bfloat16),
                grad_k.reshape(WINDOW_TOKENS, DK).astype(jnp.bfloat16), value_gradient.reshape(WINDOW_TOKENS, DV).astype(jnp.bfloat16))

    stacked = lax.map(one_head, jnp.arange(HEADS, dtype=jnp.int32))

    def merge_heads(per_head):
        return jnp.transpose(per_head, (1, 0, 2)).reshape(WINDOW_TOKENS, -1)

    return (merge_heads(stacked[0]), merge_heads(stacked[1]), merge_heads(stacked[2]), merge_heads(stacked[3]))
```

```python
import jax
import jax.numpy as jnp
from jax import lax
from jax.sharding import PartitionSpec as P

BLOCK = 128
WINDOW_BLOCKS = 16


def passed_along(block, axis, distance):
    devices = range(lax.axis_size(axis))
    route = [(i - distance, i) for i in devices if i - distance in devices]
    return lax.ppermute(block, axis, route)


def document_ids(doc_lengths, first_place, span_length):
    starts = jnp.cumsum(doc_lengths, dtype=jnp.int32) - doc_lengths
    places = first_place - 1 + jnp.arange(span_length + 1, dtype=jnp.int32)
    return jnp.sum((starts[None, :] <= places[:, None]).astype(jnp.int32), axis=1) - 1


def decay_tables(log_rates, doc_ids, block_size, score_scaling):
    block_count = log_rates.shape[0] // block_size
    cumulated = jnp.cumsum(log_rates.reshape(block_count, block_size), axis=1)
    before = doc_ids[0 : block_count * block_size : block_size]
    own_ids = doc_ids[1:].reshape(block_count, block_size)
    carried = (own_ids == before[:, None]).astype(jnp.float32)
    last_ids = own_ids[:, block_size - 1]
    tail_mask = (own_ids == last_ids[:, None]).astype(jnp.float32)
    block_decay = jnp.exp(cumulated[:, block_size - 1]) * carried[:, block_size - 1]
    row_index = lax.broadcasted_iota(jnp.int32, (block_size, block_size), 0)
    column_index = lax.broadcasted_iota(jnp.int32, (block_size, block_size), 1)
    inside = (own_ids[:, :, None] == own_ids[:, None, :]) & (row_index >= column_index)[None]
    decay_gaps = cumulated[:, :, None] - cumulated[:, None, :]
    weights = jnp.where(inside, jnp.exp(jnp.where(inside, decay_gaps, 0.0)), 0.0) * score_scaling
    per_head_decay_rate = jnp.exp(cumulated) * carried
    tail_decay = jnp.exp(cumulated[:, block_size - 1 :] - cumulated) * tail_mask
    return (weights, per_head_decay_rate, tail_decay, block_decay)


def window_product(all_decays, me, first, size):
    places = first + jnp.arange(size, dtype=jnp.int32)
    inside = (places >= 0) & (places < all_decays.shape[0])
    picked = jnp.where(inside, all_decays[jnp.clip(places, 0, all_decays.shape[0] - 1)], 1.0)
    return jnp.prod(picked)


def windowed_scan(own, all_decays, me, direction):
    current = passed_along(own, "ctx", direction)
    offset = 1
    while offset < WINDOW_BLOCKS:
        pulled = passed_along(current, "ctx", direction * offset)
        if direction > 0:
            gain = window_product(all_decays, me, me - offset, offset)
        else:
            gain = window_product(all_decays, me, me + 1, offset)
        current = gain * pulled + current
        offset *= 2
    return current


def per_device(queries, keys, values, grad_out, log_decay, doc_lengths):
    heads = lax.axis_size("head")
    rows = queries.shape[0]
    key_dim = queries.shape[1] // heads
    value_dim = values.shape[1] // heads
    packed = jnp.concatenate(
        [
            queries.reshape(rows, heads, key_dim),
            keys.reshape(rows, heads, key_dim),
            values.reshape(rows, heads, value_dim),
        ],
        axis=2,
    ).reshape(rows, heads * (2 * key_dim + value_dim))
    gathered = lax.all_to_all(packed, "head", split_axis=1, concat_axis=0, tiled=True)
    query_rows = gathered[:, :key_dim]
    key_rows = gathered[:, key_dim : 2 * key_dim]
    value_rows = gathered[:, 2 * key_dim :]
    tok_dev = key_rows.shape[0]
    block_count = tok_dev // BLOCK
    score_scaling = (key_dim * BLOCK) ** (-0.5)
    me = lax.axis_index("ctx")
    doc_ids = document_ids(doc_lengths, me * tok_dev, tok_dev)
    weights, per_head_decay_rate, tail_decay, block_decay = decay_tables(
        log_decay[0], doc_ids, BLOCK, score_scaling
    )
    all_decays = lax.all_gather(block_decay[0], "ctx")
    query_block_list = query_rows.reshape(block_count, BLOCK, key_dim)
    key_blocks = key_rows.reshape(block_count, BLOCK, key_dim)
    value_block_list = value_rows.reshape(block_count, BLOCK, value_dim)
    gradient_block_list = grad_out.reshape(block_count, BLOCK, value_dim)
    keyed_blocks = (key_blocks * tail_decay[:, :, None]).astype(jnp.bfloat16)
    updates = jnp.einsum(
        "ncd,nce->nde", keyed_blocks, value_block_list, preferred_element_type=jnp.float32
    )
    queried = (query_block_list * (per_head_decay_rate * score_scaling)[:, :, None]).astype(
        jnp.bfloat16
    )
    back_updates = jnp.einsum(
        "ncd,nce->nde", queried, gradient_block_list, preferred_element_type=jnp.float32
    )
    states = windowed_scan(updates[0], all_decays, me, 1)[None]
    ends = windowed_scan(back_updates[0], all_decays, me, -1)[None]
    lowered_state = states.astype(jnp.bfloat16)
    back_low = ends.astype(jnp.bfloat16)
    scores = jnp.einsum(
        "nid,njd->nij", query_block_list, key_blocks, preferred_element_type=jnp.float32
    )
    attention_weights = (scores * weights).astype(jnp.bfloat16)
    retained = (
        jnp.einsum(
            "xho,xoy->xhy", query_block_list, lowered_state, preferred_element_type=jnp.float32
        )
        * (per_head_decay_rate * score_scaling)[:, :, None]
    )
    retained = retained + jnp.einsum(
        "bcv,bvd->bcd", attention_weights, value_block_list, preferred_element_type=jnp.float32
    )
    score_gradient = jnp.einsum(
        "ysb,ytb->yst", gradient_block_list, value_block_list, preferred_element_type=jnp.float32
    )
    gprobs = (score_gradient * weights).astype(jnp.bfloat16)
    query_gradient = (
        jnp.einsum(
            "srj,sqj->srq", gradient_block_list, lowered_state, preferred_element_type=jnp.float32
        )
        * (per_head_decay_rate * score_scaling)[:, :, None]
    )
    query_gradient = query_gradient + jnp.einsum(
        "nij,njd->nid", gprobs, key_blocks, preferred_element_type=jnp.float32
    )
    grad_k = (
        jnp.einsum("nje,nde->njd", value_block_list, back_low, preferred_element_type=jnp.float32)
        * tail_decay[:, :, None]
    )
    grad_k = grad_k + jnp.einsum(
        "nij,nid->njd", gprobs, query_block_list, preferred_element_type=jnp.float32
    )
    value_gradient = (
        jnp.einsum("njd,nde->nje", key_blocks, back_low, preferred_element_type=jnp.float32)
        * tail_decay[:, :, None]
    )
    value_gradient = value_gradient + jnp.einsum(
        "glu,glx->gux", attention_weights, gradient_block_list, preferred_element_type=jnp.float32
    )
    return (
        retained.reshape(tok_dev, value_dim).astype(jnp.bfloat16),
        query_gradient.reshape(tok_dev, key_dim).astype(jnp.bfloat16),
        grad_k.reshape(tok_dev, key_dim).astype(jnp.bfloat16),
        value_gradient.reshape(tok_dev, value_dim).astype(jnp.bfloat16),
    )


def solution(mesh):
    placed = (
        P(("ctx", "head"), None),
        P(("ctx", "head"), None),
        P(("ctx", "head"), None),
        P("ctx", "head"),
        P("head", "ctx"),
        P(),
    )
    return jax.shard_map(
        per_device,
        mesh=mesh,
        in_specs=placed,
        out_specs=(P("ctx", "head"), P("ctx", "head"), P("ctx", "head"), P("ctx", "head")),
        check_vma=False,
    )
```

```python
import jax
import jax.numpy as jnp
from jax import lax
from jax.sharding import PartitionSpec as P

BLOCK = 128
WINDOW_BLOCKS = 16


def passed_along(block, axis, distance):
    devices = range(lax.axis_size(axis))
    route = [(i - distance, i) for i in devices if i - distance in devices]
    return lax.ppermute(block, axis, route)


def document_ids(doc_lengths, first_place, span_length):
    starts = jnp.cumsum(doc_lengths, dtype=jnp.int32) - doc_lengths
    places = first_place - 1 + jnp.arange(span_length + 1, dtype=jnp.int32)
    return jnp.sum((starts[None, :] <= places[:, None]).astype(jnp.int32), axis=1) - 1


def decay_tables(log_rates, doc_ids, block_size, score_scaling):
    block_count = log_rates.shape[0] // block_size
    cumulated = jnp.cumsum(log_rates.reshape(block_count, block_size), axis=1)
    before = doc_ids[0 : block_count * block_size : block_size]
    own_ids = doc_ids[1:].reshape(block_count, block_size)
    carried = (own_ids == before[:, None]).astype(jnp.float32)
    last_ids = own_ids[:, block_size - 1]
    tail_mask = (own_ids == last_ids[:, None]).astype(jnp.float32)
    block_decay = jnp.exp(cumulated[:, block_size - 1]) * carried[:, block_size - 1]
    row_index = lax.broadcasted_iota(jnp.int32, (block_size, block_size), 0)
    column_index = lax.broadcasted_iota(jnp.int32, (block_size, block_size), 1)
    inside = (own_ids[:, :, None] == own_ids[:, None, :]) & (row_index >= column_index)[None]
    decay_gaps = cumulated[:, :, None] - cumulated[:, None, :]
    weights = jnp.where(inside, jnp.exp(jnp.where(inside, decay_gaps, 0.0)), 0.0) * score_scaling
    per_head_decay_rate = jnp.exp(cumulated) * carried
    tail_decay = jnp.exp(cumulated[:, block_size - 1 :] - cumulated) * tail_mask
    return (weights, per_head_decay_rate, tail_decay, block_decay)


def windowed_scan(own, own_decay, direction):
    rows, cols = own.shape
    gain_rows = jnp.broadcast_to(own_decay, (8, cols)).astype(own.dtype)
    message = jnp.concatenate([own, gain_rows], axis=0)
    keep = (lax.broadcasted_iota(jnp.int32, (rows + 8, 1), 0) < rows).astype(own.dtype)
    current = passed_along(message, "ctx", direction)
    offset = 1
    while offset < WINDOW_BLOCKS:
        pulled = passed_along(current, "ctx", direction * offset)
        gain = current[rows, 0]
        current = gain * pulled + current * keep
        offset *= 2
    return current[:rows]


def per_device(queries, keys, values, grad_out, log_decay, doc_lengths):
    heads = lax.axis_size("head")
    rows = queries.shape[0]
    key_dim = queries.shape[1] // heads
    value_dim = values.shape[1] // heads
    packed = jnp.concatenate(
        [
            queries.reshape(rows, heads, key_dim),
            keys.reshape(rows, heads, key_dim),
            values.reshape(rows, heads, value_dim),
        ],
        axis=2,
    ).reshape(rows, heads * (2 * key_dim + value_dim))
    gathered = lax.all_to_all(packed, "head", split_axis=1, concat_axis=0, tiled=True)
    query_rows = gathered[:, :key_dim]
    key_rows = gathered[:, key_dim : 2 * key_dim]
    value_rows = gathered[:, 2 * key_dim :]
    tok_dev = key_rows.shape[0]
    block_count = tok_dev // BLOCK
    score_scaling = (key_dim * BLOCK) ** (-0.5)
    me = lax.axis_index("ctx")
    doc_ids = document_ids(doc_lengths, me * tok_dev, tok_dev)
    weights, per_head_decay_rate, tail_decay, block_decay = decay_tables(
        log_decay[0], doc_ids, BLOCK, score_scaling
    )
    query_block_list = query_rows.reshape(block_count, BLOCK, key_dim)
    key_blocks = key_rows.reshape(block_count, BLOCK, key_dim)
    value_block_list = value_rows.reshape(block_count, BLOCK, value_dim)
    gradient_block_list = grad_out.reshape(block_count, BLOCK, value_dim)
    keyed_blocks = (key_blocks * tail_decay[:, :, None]).astype(jnp.bfloat16)
    updates = jnp.einsum(
        "ncd,nce->nde", keyed_blocks, value_block_list, preferred_element_type=jnp.float32
    )
    queried = (query_block_list * (per_head_decay_rate * score_scaling)[:, :, None]).astype(
        jnp.bfloat16
    )
    back_updates = jnp.einsum(
        "ncd,nce->nde", queried, gradient_block_list, preferred_element_type=jnp.float32
    )
    states = windowed_scan(updates[0], block_decay[0], 1)[None]
    ends = windowed_scan(back_updates[0], block_decay[0], -1)[None]
    lowered_state = states.astype(jnp.bfloat16)
    back_low = ends.astype(jnp.bfloat16)
    scores = jnp.einsum(
        "nid,njd->nij", query_block_list, key_blocks, preferred_element_type=jnp.float32
    )
    attention_weights = (scores * weights).astype(jnp.bfloat16)
    retained = (
        jnp.einsum(
            "xho,xoy->xhy", query_block_list, lowered_state, preferred_element_type=jnp.float32
        )
        * (per_head_decay_rate * score_scaling)[:, :, None]
    )
    retained = retained + jnp.einsum(
        "bcv,bvd->bcd", attention_weights, value_block_list, preferred_element_type=jnp.float32
    )
    score_gradient = jnp.einsum(
        "ysb,ytb->yst", gradient_block_list, value_block_list, preferred_element_type=jnp.float32
    )
    gprobs = (score_gradient * weights).astype(jnp.bfloat16)
    query_gradient = (
        jnp.einsum(
            "srj,sqj->srq", gradient_block_list, lowered_state, preferred_element_type=jnp.float32
        )
        * (per_head_decay_rate * score_scaling)[:, :, None]
    )
    query_gradient = query_gradient + jnp.einsum(
        "nij,njd->nid", gprobs, key_blocks, preferred_element_type=jnp.float32
    )
    grad_k = (
        jnp.einsum("nje,nde->njd", value_block_list, back_low, preferred_element_type=jnp.float32)
        * tail_decay[:, :, None]
    )
    grad_k = grad_k + jnp.einsum(
        "nij,nid->njd", gprobs, query_block_list, preferred_element_type=jnp.float32
    )
    value_gradient = (
        jnp.einsum("njd,nde->nje", key_blocks, back_low, preferred_element_type=jnp.float32)
        * tail_decay[:, :, None]
    )
    value_gradient = value_gradient + jnp.einsum(
        "glu,glx->gux", attention_weights, gradient_block_list, preferred_element_type=jnp.float32
    )
    return (
        retained.reshape(tok_dev, value_dim).astype(jnp.bfloat16),
        query_gradient.reshape(tok_dev, key_dim).astype(jnp.bfloat16),
        grad_k.reshape(tok_dev, key_dim).astype(jnp.bfloat16),
        value_gradient.reshape(tok_dev, value_dim).astype(jnp.bfloat16),
    )


def solution(mesh):
    placed = (
        P(("ctx", "head"), None),
        P(("ctx", "head"), None),
        P(("ctx", "head"), None),
        P("ctx", "head"),
        P("head", "ctx"),
        P(),
    )
    return jax.shard_map(
        per_device,
        mesh=mesh,
        in_specs=placed,
        out_specs=(P("ctx", "head"), P("ctx", "head"), P("ctx", "head"), P("ctx", "head")),
        check_vma=False,
    )
```

```python
import jax
import jax.numpy as jnp
from jax import lax
from jax.sharding import PartitionSpec as P

BLOCK = 128
WINDOW_BLOCKS = 16


def passed_along(block, axis, distance):
    devices = range(lax.axis_size(axis))
    route = [(i - distance, i) for i in devices if i - distance in devices]
    return lax.ppermute(block, axis, route)


def document_ids(doc_lengths, first_place, span_length):
    starts = jnp.cumsum(doc_lengths, dtype=jnp.int32) - doc_lengths
    places = first_place - 1 + jnp.arange(span_length + 1, dtype=jnp.int32)
    return jnp.sum((starts[None, :] <= places[:, None]).astype(jnp.int32), axis=1) - 1


def decay_tables(log_rates, doc_ids, block_size, score_scaling):
    block_count = log_rates.shape[0] // block_size
    cumulated = jnp.cumsum(log_rates.reshape(block_count, block_size), axis=1)
    before = doc_ids[0 : block_count * block_size : block_size]
    own_ids = doc_ids[1:].reshape(block_count, block_size)
    carried = (own_ids == before[:, None]).astype(jnp.float32)
    last_ids = own_ids[:, block_size - 1]
    tail_mask = (own_ids == last_ids[:, None]).astype(jnp.float32)
    block_decay = jnp.exp(cumulated[:, block_size - 1]) * carried[:, block_size - 1]
    row_index = lax.broadcasted_iota(jnp.int32, (block_size, block_size), 0)
    column_index = lax.broadcasted_iota(jnp.int32, (block_size, block_size), 1)
    inside = (own_ids[:, :, None] == own_ids[:, None, :]) & (row_index >= column_index)[None]
    decay_gaps = cumulated[:, :, None] - cumulated[:, None, :]
    weights = jnp.where(inside, jnp.exp(jnp.where(inside, decay_gaps, 0.0)), 0.0) * score_scaling
    per_head_decay_rate = jnp.exp(cumulated) * carried
    tail_decay = jnp.exp(cumulated[:, block_size - 1 :] - cumulated) * tail_mask
    return (weights, per_head_decay_rate, tail_decay, block_decay)


RELAY_BLOCKS = WINDOW_BLOCKS // 2


def neighbour_decays(own_decay, direction):
    known = passed_along(own_decay.reshape(1), "ctx", direction)
    while known.shape[0] < RELAY_BLOCKS:
        far = passed_along(known, "ctx", direction * known.shape[0])
        known = jnp.concatenate([known, far])
    return known


def relayed_partial(bundle, decays, split, direction):
    received = []
    moving = bundle
    for _ in range(RELAY_BLOCKS):
        moving = passed_along(moving, "ctx", direction)
        received.append(moving)
    stacked = jnp.stack(received)
    updates = jnp.einsum(
        "kcd,kce->kde",
        stacked[:, :, :split],
        stacked[:, :, split:],
        preferred_element_type=jnp.float32,
    )
    acc = updates[RELAY_BLOCKS - 1]
    for k in range(RELAY_BLOCKS - 1, 0, -1):
        acc = decays[k - 1] * acc + updates[k - 1]
    gain = decays[0]
    for k in range(1, RELAY_BLOCKS):
        gain = gain * decays[k]
    joined = passed_along(acc, "ctx", direction * RELAY_BLOCKS)
    return gain * joined + acc


def per_device(queries, keys, values, grad_out, log_decay, doc_lengths):
    heads = lax.axis_size("head")
    rows = queries.shape[0]
    key_dim = queries.shape[1] // heads
    value_dim = values.shape[1] // heads
    packed = jnp.concatenate(
        [
            queries.reshape(rows, heads, key_dim),
            keys.reshape(rows, heads, key_dim),
            values.reshape(rows, heads, value_dim),
        ],
        axis=2,
    ).reshape(rows, heads * (2 * key_dim + value_dim))
    gathered = lax.all_to_all(packed, "head", split_axis=1, concat_axis=0, tiled=True)
    query_rows = gathered[:, :key_dim]
    key_rows = gathered[:, key_dim : 2 * key_dim]
    value_rows = gathered[:, 2 * key_dim :]
    tok_dev = key_rows.shape[0]
    block_count = tok_dev // BLOCK
    score_scaling = (key_dim * BLOCK) ** (-0.5)
    me = lax.axis_index("ctx")
    doc_ids = document_ids(doc_lengths, me * tok_dev, tok_dev)
    weights, per_head_decay_rate, tail_decay, block_decay = decay_tables(
        log_decay[0], doc_ids, BLOCK, score_scaling
    )
    query_block_list = query_rows.reshape(block_count, BLOCK, key_dim)
    key_blocks = key_rows.reshape(block_count, BLOCK, key_dim)
    value_block_list = value_rows.reshape(block_count, BLOCK, value_dim)
    gradient_block_list = grad_out.reshape(block_count, BLOCK, value_dim)
    keyed_blocks = (key_blocks * tail_decay[:, :, None]).astype(jnp.bfloat16)
    queried = (query_block_list * (per_head_decay_rate * score_scaling)[:, :, None]).astype(
        jnp.bfloat16
    )
    earlier_decays = neighbour_decays(block_decay[0], 1)
    later_decays = neighbour_decays(block_decay[0], -1)
    forward_bundle = jnp.concatenate([keyed_blocks[0], value_block_list[0]], axis=1)
    backward_bundle = jnp.concatenate([queried[0], gradient_block_list[0]], axis=1)
    states = relayed_partial(forward_bundle, earlier_decays, key_dim, 1)[None]
    ends = relayed_partial(backward_bundle, later_decays, key_dim, -1)[None]
    lowered_state = states.astype(jnp.bfloat16)
    back_low = ends.astype(jnp.bfloat16)
    scores = jnp.einsum(
        "nid,njd->nij", query_block_list, key_blocks, preferred_element_type=jnp.float32
    )
    attention_weights = (scores * weights).astype(jnp.bfloat16)
    retained = (
        jnp.einsum(
            "xho,xoy->xhy", query_block_list, lowered_state, preferred_element_type=jnp.float32
        )
        * (per_head_decay_rate * score_scaling)[:, :, None]
    )
    retained = retained + jnp.einsum(
        "bcv,bvd->bcd", attention_weights, value_block_list, preferred_element_type=jnp.float32
    )
    score_gradient = jnp.einsum(
        "ysb,ytb->yst", gradient_block_list, value_block_list, preferred_element_type=jnp.float32
    )
    gprobs = (score_gradient * weights).astype(jnp.bfloat16)
    query_gradient = (
        jnp.einsum(
            "srj,sqj->srq", gradient_block_list, lowered_state, preferred_element_type=jnp.float32
        )
        * (per_head_decay_rate * score_scaling)[:, :, None]
    )
    query_gradient = query_gradient + jnp.einsum(
        "nij,njd->nid", gprobs, key_blocks, preferred_element_type=jnp.float32
    )
    grad_k = (
        jnp.einsum("nje,nde->njd", value_block_list, back_low, preferred_element_type=jnp.float32)
        * tail_decay[:, :, None]
    )
    grad_k = grad_k + jnp.einsum(
        "nij,nid->njd", gprobs, query_block_list, preferred_element_type=jnp.float32
    )
    value_gradient = (
        jnp.einsum("njd,nde->nje", key_blocks, back_low, preferred_element_type=jnp.float32)
        * tail_decay[:, :, None]
    )
    value_gradient = value_gradient + jnp.einsum(
        "glu,glx->gux", attention_weights, gradient_block_list, preferred_element_type=jnp.float32
    )
    return (
        retained.reshape(tok_dev, value_dim).astype(jnp.bfloat16),
        query_gradient.reshape(tok_dev, key_dim).astype(jnp.bfloat16),
        grad_k.reshape(tok_dev, key_dim).astype(jnp.bfloat16),
        value_gradient.reshape(tok_dev, value_dim).astype(jnp.bfloat16),
    )


def solution(mesh):
    placed = (
        P(("ctx", "head"), None),
        P(("ctx", "head"), None),
        P(("ctx", "head"), None),
        P("ctx", "head"),
        P("head", "ctx"),
        P(),
    )
    return jax.shard_map(
        per_device,
        mesh=mesh,
        in_specs=placed,
        out_specs=(P("ctx", "head"), P("ctx", "head"), P("ctx", "head"), P("ctx", "head")),
        check_vma=False,
    )
```

```python
import jax
import jax.numpy as jnp
from jax import lax
from jax.sharding import PartitionSpec as P

BLOCK = 128
WINDOW_BLOCKS = 16


def passed_along(block, axis, distance):
    devices = range(lax.axis_size(axis))
    route = [(i - distance, i) for i in devices if i - distance in devices]
    return lax.ppermute(block, axis, route)


def document_ids(doc_lengths, first_place, span_length):
    starts = jnp.cumsum(doc_lengths, dtype=jnp.int32) - doc_lengths
    places = first_place - 1 + jnp.arange(span_length + 1, dtype=jnp.int32)
    return jnp.sum((starts[None, :] <= places[:, None]).astype(jnp.int32), axis=1) - 1


def decay_tables(log_rates, doc_ids, block_size, score_scaling):
    block_count = log_rates.shape[0] // block_size
    cumulated = jnp.cumsum(log_rates.reshape(block_count, block_size), axis=1)
    before = doc_ids[0 : block_count * block_size : block_size]
    own_ids = doc_ids[1:].reshape(block_count, block_size)
    carried = (own_ids == before[:, None]).astype(jnp.float32)
    last_ids = own_ids[:, block_size - 1]
    tail_mask = (own_ids == last_ids[:, None]).astype(jnp.float32)
    block_decay = jnp.exp(cumulated[:, block_size - 1]) * carried[:, block_size - 1]
    row_index = lax.broadcasted_iota(jnp.int32, (block_size, block_size), 0)
    column_index = lax.broadcasted_iota(jnp.int32, (block_size, block_size), 1)
    inside = (own_ids[:, :, None] == own_ids[:, None, :]) & (row_index >= column_index)[None]
    decay_gaps = cumulated[:, :, None] - cumulated[:, None, :]
    weights = jnp.where(inside, jnp.exp(jnp.where(inside, decay_gaps, 0.0)), 0.0) * score_scaling
    per_head_decay_rate = jnp.exp(cumulated) * carried
    tail_decay = jnp.exp(cumulated[:, block_size - 1 :] - cumulated) * tail_mask
    return (weights, per_head_decay_rate, tail_decay, block_decay)


RELAY_BLOCKS = WINDOW_BLOCKS // 2
GAIN_ROWS = 8


def pieces_of(decay):
    high = lax.reduce_precision(decay, exponent_bits=8, mantissa_bits=7)
    rest = decay - high
    middle = lax.reduce_precision(rest, exponent_bits=8, mantissa_bits=7)
    return jnp.stack([high, middle, rest - middle])


def relayed_partial(left, right, own_decay, direction):
    rows = left.shape[0]
    split = left.shape[1]
    cols = split + right.shape[1]
    parts = jnp.zeros((GAIN_ROWS, cols), jnp.float32).at[:3, :].set(pieces_of(own_decay)[:, None])
    moving = jnp.concatenate(
        [jnp.concatenate([left, right], axis=1), parts.astype(jnp.bfloat16)], axis=0
    )
    acc = None
    gain = None
    for _ in range(RELAY_BLOCKS):
        moving = passed_along(moving, "ctx", direction)
        update = jnp.einsum(
            "cd,ce->de",
            moving[:rows, :split],
            moving[:rows, split:],
            preferred_element_type=jnp.float32,
        )
        coded = moving[rows : rows + 3, 0].astype(jnp.float32)
        decay = (coded[0] + coded[1]) + coded[2]
        if acc is None:
            acc = update
            gain = decay
        else:
            acc = acc + gain * update
            gain = gain * decay
    joined = passed_along(acc, "ctx", direction * RELAY_BLOCKS)
    return gain * joined + acc


def per_device(queries, keys, values, grad_out, log_decay, doc_lengths):
    heads = lax.axis_size("head")
    rows = queries.shape[0]
    key_dim = queries.shape[1] // heads
    value_dim = values.shape[1] // heads
    packed = jnp.concatenate(
        [
            queries.reshape(rows, heads, key_dim),
            keys.reshape(rows, heads, key_dim),
            values.reshape(rows, heads, value_dim),
        ],
        axis=2,
    ).reshape(rows, heads * (2 * key_dim + value_dim))
    gathered = lax.all_to_all(packed, "head", split_axis=1, concat_axis=0, tiled=True)
    query_rows = gathered[:, :key_dim]
    key_rows = gathered[:, key_dim : 2 * key_dim]
    value_rows = gathered[:, 2 * key_dim :]
    tok_dev = key_rows.shape[0]
    block_count = tok_dev // BLOCK
    score_scaling = (key_dim * BLOCK) ** (-0.5)
    me = lax.axis_index("ctx")
    doc_ids = document_ids(doc_lengths, me * tok_dev, tok_dev)
    weights, per_head_decay_rate, tail_decay, block_decay = decay_tables(
        log_decay[0], doc_ids, BLOCK, score_scaling
    )
    query_block_list = query_rows.reshape(block_count, BLOCK, key_dim)
    key_blocks = key_rows.reshape(block_count, BLOCK, key_dim)
    value_block_list = value_rows.reshape(block_count, BLOCK, value_dim)
    gradient_block_list = grad_out.reshape(block_count, BLOCK, value_dim)
    keyed_blocks = (key_blocks * tail_decay[:, :, None]).astype(jnp.bfloat16)
    queried = (query_block_list * (per_head_decay_rate * score_scaling)[:, :, None]).astype(
        jnp.bfloat16
    )
    states = relayed_partial(keyed_blocks[0], value_block_list[0], block_decay[0], 1)[None]
    ends = relayed_partial(queried[0], gradient_block_list[0], block_decay[0], -1)[None]
    lowered_state = states.astype(jnp.bfloat16)
    back_low = ends.astype(jnp.bfloat16)
    scores = jnp.einsum(
        "nid,njd->nij", query_block_list, key_blocks, preferred_element_type=jnp.float32
    )
    attention_weights = (scores * weights).astype(jnp.bfloat16)
    retained = (
        jnp.einsum(
            "xho,xoy->xhy", query_block_list, lowered_state, preferred_element_type=jnp.float32
        )
        * (per_head_decay_rate * score_scaling)[:, :, None]
    )
    retained = retained + jnp.einsum(
        "bcv,bvd->bcd", attention_weights, value_block_list, preferred_element_type=jnp.float32
    )
    score_gradient = jnp.einsum(
        "ysb,ytb->yst", gradient_block_list, value_block_list, preferred_element_type=jnp.float32
    )
    gprobs = (score_gradient * weights).astype(jnp.bfloat16)
    query_gradient = (
        jnp.einsum(
            "srj,sqj->srq", gradient_block_list, lowered_state, preferred_element_type=jnp.float32
        )
        * (per_head_decay_rate * score_scaling)[:, :, None]
    )
    query_gradient = query_gradient + jnp.einsum(
        "nij,njd->nid", gprobs, key_blocks, preferred_element_type=jnp.float32
    )
    grad_k = (
        jnp.einsum("nje,nde->njd", value_block_list, back_low, preferred_element_type=jnp.float32)
        * tail_decay[:, :, None]
    )
    grad_k = grad_k + jnp.einsum(
        "nij,nid->njd", gprobs, query_block_list, preferred_element_type=jnp.float32
    )
    value_gradient = (
        jnp.einsum("njd,nde->nje", key_blocks, back_low, preferred_element_type=jnp.float32)
        * tail_decay[:, :, None]
    )
    value_gradient = value_gradient + jnp.einsum(
        "glu,glx->gux", attention_weights, gradient_block_list, preferred_element_type=jnp.float32
    )
    return (
        retained.reshape(tok_dev, value_dim).astype(jnp.bfloat16),
        query_gradient.reshape(tok_dev, key_dim).astype(jnp.bfloat16),
        grad_k.reshape(tok_dev, key_dim).astype(jnp.bfloat16),
        value_gradient.reshape(tok_dev, value_dim).astype(jnp.bfloat16),
    )


def solution(mesh):
    placed = (
        P(("ctx", "head"), None),
        P(("ctx", "head"), None),
        P(("ctx", "head"), None),
        P("ctx", "head"),
        P("head", "ctx"),
        P(),
    )
    return jax.shard_map(
        per_device,
        mesh=mesh,
        in_specs=placed,
        out_specs=(P("ctx", "head"), P("ctx", "head"), P("ctx", "head"), P("ctx", "head")),
        check_vma=False,
    )
```

```python
import jax
import jax.numpy as jnp
from jax import lax
from jax.sharding import PartitionSpec as P

BLOCK = 128
WINDOW_BLOCKS = 16


def passed_along(block, axis, distance):
    devices = range(lax.axis_size(axis))
    route = [(i - distance, i) for i in devices if i - distance in devices]
    return lax.ppermute(block, axis, route)


def document_ids(doc_lengths, first_place, span_length):
    starts = jnp.cumsum(doc_lengths, dtype=jnp.int32) - doc_lengths
    places = first_place - 1 + jnp.arange(span_length + 1, dtype=jnp.int32)
    return jnp.sum((starts[None, :] <= places[:, None]).astype(jnp.int32), axis=1) - 1


def decay_tables(log_rates, doc_ids, block_size, score_scaling):
    block_count = log_rates.shape[0] // block_size
    cumulated = jnp.cumsum(log_rates.reshape(block_count, block_size), axis=1)
    before = doc_ids[0 : block_count * block_size : block_size]
    own_ids = doc_ids[1:].reshape(block_count, block_size)
    carried = (own_ids == before[:, None]).astype(jnp.float32)
    last_ids = own_ids[:, block_size - 1]
    tail_mask = (own_ids == last_ids[:, None]).astype(jnp.float32)
    block_decay = jnp.exp(cumulated[:, block_size - 1]) * carried[:, block_size - 1]
    row_index = lax.broadcasted_iota(jnp.int32, (block_size, block_size), 0)
    column_index = lax.broadcasted_iota(jnp.int32, (block_size, block_size), 1)
    inside = (own_ids[:, :, None] == own_ids[:, None, :]) & (row_index >= column_index)[None]
    decay_gaps = cumulated[:, :, None] - cumulated[:, None, :]
    weights = jnp.where(inside, jnp.exp(jnp.where(inside, decay_gaps, 0.0)), 0.0) * score_scaling
    per_head_decay_rate = jnp.exp(cumulated) * carried
    tail_decay = jnp.exp(cumulated[:, block_size - 1 :] - cumulated) * tail_mask
    return (weights, per_head_decay_rate, tail_decay, block_decay)


RELAY_BLOCKS = WINDOW_BLOCKS // 2
GAIN_ROWS = 8


def pieces_of(decay):
    high = lax.reduce_precision(decay, exponent_bits=8, mantissa_bits=7)
    rest = decay - high
    middle = lax.reduce_precision(rest, exponent_bits=8, mantissa_bits=7)
    return jnp.stack([high, middle, rest - middle])


def relayed_partial(left, right, own_decay, direction):
    rows = left.shape[0]
    split = left.shape[1]
    cols = split + right.shape[1]
    parts = jnp.zeros((GAIN_ROWS, cols), jnp.float32).at[:3, :].set(pieces_of(own_decay)[:, None])
    moving = jnp.concatenate(
        [jnp.concatenate([left, right], axis=1), parts.astype(jnp.bfloat16)], axis=0
    )
    received = []
    for _ in range(RELAY_BLOCKS):
        moving = passed_along(moving, "ctx", direction)
        received.append(moving)
    stacked = jnp.stack(received)
    updates = jnp.einsum(
        "kcd,kce->kde",
        stacked[:, :rows, :split],
        stacked[:, :rows, split:],
        preferred_element_type=jnp.float32,
    )
    coded = stacked[:, rows : rows + 3, 0].astype(jnp.float32)
    decays = (coded[:, 0] + coded[:, 1]) + coded[:, 2]
    weights = [jnp.float32(1.0)]
    for k in range(1, RELAY_BLOCKS + 1):
        weights.append(weights[-1] * decays[k - 1])
    gain = weights[RELAY_BLOCKS]
    acc = updates[0]
    for k in range(1, RELAY_BLOCKS):
        acc = acc + weights[k] * updates[k]
    joined = passed_along(acc, "ctx", direction * RELAY_BLOCKS)
    return gain * joined + acc


def per_device(queries, keys, values, grad_out, log_decay, doc_lengths):
    heads = lax.axis_size("head")
    rows = queries.shape[0]
    key_dim = queries.shape[1] // heads
    value_dim = values.shape[1] // heads
    packed = jnp.concatenate(
        [
            queries.reshape(rows, heads, key_dim),
            keys.reshape(rows, heads, key_dim),
            values.reshape(rows, heads, value_dim),
        ],
        axis=2,
    ).reshape(rows, heads * (2 * key_dim + value_dim))
    gathered = lax.all_to_all(packed, "head", split_axis=1, concat_axis=0, tiled=True)
    query_rows = gathered[:, :key_dim]
    key_rows = gathered[:, key_dim : 2 * key_dim]
    value_rows = gathered[:, 2 * key_dim :]
    tok_dev = key_rows.shape[0]
    block_count = tok_dev // BLOCK
    score_scaling = (key_dim * BLOCK) ** (-0.5)
    me = lax.axis_index("ctx")
    doc_ids = document_ids(doc_lengths, me * tok_dev, tok_dev)
    weights, per_head_decay_rate, tail_decay, block_decay = decay_tables(
        log_decay[0], doc_ids, BLOCK, score_scaling
    )
    query_block_list = query_rows.reshape(block_count, BLOCK, key_dim)
    key_blocks = key_rows.reshape(block_count, BLOCK, key_dim)
    value_block_list = value_rows.reshape(block_count, BLOCK, value_dim)
    gradient_block_list = grad_out.reshape(block_count, BLOCK, value_dim)
    keyed_blocks = (key_blocks * tail_decay[:, :, None]).astype(jnp.bfloat16)
    queried = (query_block_list * (per_head_decay_rate * score_scaling)[:, :, None]).astype(
        jnp.bfloat16
    )
    states = relayed_partial(keyed_blocks[0], value_block_list[0], block_decay[0], 1)[None]
    ends = relayed_partial(queried[0], gradient_block_list[0], block_decay[0], -1)[None]
    lowered_state = states.astype(jnp.bfloat16)
    back_low = ends.astype(jnp.bfloat16)
    scores = jnp.einsum(
        "nid,njd->nij", query_block_list, key_blocks, preferred_element_type=jnp.float32
    )
    attention_weights = (scores * weights).astype(jnp.bfloat16)
    retained = (
        jnp.einsum(
            "xho,xoy->xhy", query_block_list, lowered_state, preferred_element_type=jnp.float32
        )
        * (per_head_decay_rate * score_scaling)[:, :, None]
    )
    retained = retained + jnp.einsum(
        "bcv,bvd->bcd", attention_weights, value_block_list, preferred_element_type=jnp.float32
    )
    score_gradient = jnp.einsum(
        "ysb,ytb->yst", gradient_block_list, value_block_list, preferred_element_type=jnp.float32
    )
    gprobs = (score_gradient * weights).astype(jnp.bfloat16)
    query_gradient = (
        jnp.einsum(
            "srj,sqj->srq", gradient_block_list, lowered_state, preferred_element_type=jnp.float32
        )
        * (per_head_decay_rate * score_scaling)[:, :, None]
    )
    query_gradient = query_gradient + jnp.einsum(
        "nij,njd->nid", gprobs, key_blocks, preferred_element_type=jnp.float32
    )
    grad_k = (
        jnp.einsum("nje,nde->njd", value_block_list, back_low, preferred_element_type=jnp.float32)
        * tail_decay[:, :, None]
    )
    grad_k = grad_k + jnp.einsum(
        "nij,nid->njd", gprobs, query_block_list, preferred_element_type=jnp.float32
    )
    value_gradient = (
        jnp.einsum("njd,nde->nje", key_blocks, back_low, preferred_element_type=jnp.float32)
        * tail_decay[:, :, None]
    )
    value_gradient = value_gradient + jnp.einsum(
        "glu,glx->gux", attention_weights, gradient_block_list, preferred_element_type=jnp.float32
    )
    return (
        retained.reshape(tok_dev, value_dim).astype(jnp.bfloat16),
        query_gradient.reshape(tok_dev, key_dim).astype(jnp.bfloat16),
        grad_k.reshape(tok_dev, key_dim).astype(jnp.bfloat16),
        value_gradient.reshape(tok_dev, value_dim).astype(jnp.bfloat16),
    )


def solution(mesh):
    placed = (
        P(("ctx", "head"), None),
        P(("ctx", "head"), None),
        P(("ctx", "head"), None),
        P("ctx", "head"),
        P("head", "ctx"),
        P(),
    )
    return jax.shard_map(
        per_device,
        mesh=mesh,
        in_specs=placed,
        out_specs=(P("ctx", "head"), P("ctx", "head"), P("ctx", "head"), P("ctx", "head")),
        check_vma=False,
    )
```

```python
import jax
import jax.numpy as jnp
from jax import lax
from jax.sharding import Mesh, PartitionSpec as P

BLOCK = 128
WINDOW_BLOCKS = 16


def passed_along(block, axis, distance):
    devices = range(lax.axis_size(axis))
    route = [(i - distance, i) for i in devices if i - distance in devices]
    return lax.ppermute(block, axis, route)


def document_ids(doc_lengths, first_place, span_length):
    starts = jnp.cumsum(doc_lengths, dtype=jnp.int32) - doc_lengths
    places = first_place - 1 + jnp.arange(span_length + 1, dtype=jnp.int32)
    return jnp.sum((starts[None, :] <= places[:, None]).astype(jnp.int32), axis=1) - 1


def decay_tables(log_rates, doc_ids, block_size, score_scaling):
    block_count = log_rates.shape[0] // block_size
    cumulated = jnp.cumsum(log_rates.reshape(block_count, block_size), axis=1)
    before = doc_ids[0 : block_count * block_size : block_size]
    own_ids = doc_ids[1:].reshape(block_count, block_size)
    carried = (own_ids == before[:, None]).astype(jnp.float32)
    last_ids = own_ids[:, block_size - 1]
    tail_mask = (own_ids == last_ids[:, None]).astype(jnp.float32)
    block_decay = jnp.exp(cumulated[:, block_size - 1]) * carried[:, block_size - 1]
    row_index = lax.broadcasted_iota(jnp.int32, (block_size, block_size), 0)
    column_index = lax.broadcasted_iota(jnp.int32, (block_size, block_size), 1)
    inside = (own_ids[:, :, None] == own_ids[:, None, :]) & (row_index >= column_index)[None]
    decay_gaps = cumulated[:, :, None] - cumulated[:, None, :]
    weights = jnp.where(inside, jnp.exp(jnp.where(inside, decay_gaps, 0.0)), 0.0) * score_scaling
    per_head_decay_rate = jnp.exp(cumulated) * carried
    tail_decay = jnp.exp(cumulated[:, block_size - 1 :] - cumulated) * tail_mask
    return (weights, per_head_decay_rate, tail_decay, block_decay)


RELAY_BLOCKS = WINDOW_BLOCKS // 2
GAIN_ROWS = 8


def pieces_of(decay):
    high = lax.reduce_precision(decay, exponent_bits=8, mantissa_bits=7)
    rest = decay - high
    middle = lax.reduce_precision(rest, exponent_bits=8, mantissa_bits=7)
    return jnp.stack([high, middle, rest - middle])


def coded_bundle(left, right, own_decay):
    cols = left.shape[1] + right.shape[1]
    parts = jnp.zeros((GAIN_ROWS, cols), jnp.float32).at[:3, :].set(pieces_of(own_decay)[:, None])
    return jnp.concatenate(
        [jnp.concatenate([left, right], axis=1), parts.astype(jnp.bfloat16)], axis=0
    )


def row_updates(bundles, which, rows, split):
    updates = [
        jnp.einsum(
            "cd,ce->de",
            bundles[k, which, :rows, :split],
            bundles[k, which, :rows, split:],
            preferred_element_type=jnp.float32,
        )
        for k in range(bundles.shape[0])
    ]
    coded = bundles[:, 0, rows : rows + 3, 0].astype(jnp.float32)
    decays = (coded[:, 0] + coded[:, 1]) + coded[:, 2]
    return updates, decays


def shift_x(block, distance):
    return passed_along(block, "cx", distance)


def weighted_sum(weights, updates):
    total = weights[0] * updates[0]
    for k in range(1, len(updates)):
        total = total + weights[k] * updates[k]
    return total


def forward_states(updates, decays, y):
    count = len(updates)
    w_pre = [None] * count
    w_suf = [None] * count
    run_pre = jnp.float32(1.0)
    run_suf = jnp.float32(1.0)
    for c in range(count - 1, -1, -1):
        before = c < y
        w_pre[c] = jnp.where(before, run_pre, 0.0)
        w_suf[c] = jnp.where(before, 0.0, run_suf)
        run_pre = run_pre * jnp.where(before, decays[c], 1.0)
        run_suf = run_suf * jnp.where(before, 1.0, decays[c])
    pre = weighted_sum(w_pre, updates)
    suf = weighted_sum(w_suf, updates)
    gain_pre = run_pre
    gain_suf = run_suf
    gain_row = gain_pre * gain_suf
    row = gain_suf * pre + suf
    from_two_back = shift_x(suf, 1)
    through = shift_x(gain_row * from_two_back + row, 1)
    return gain_pre * through + pre


def backward_states(updates, decays, y):
    count = len(updates)
    w_pre = [None] * count
    w_suf = [None] * count
    run_pre = jnp.float32(1.0)
    run_suf = jnp.float32(1.0)
    for c in range(count):
        after = c > y
        w_pre[c] = jnp.where(after, 0.0, run_pre)
        w_suf[c] = jnp.where(after, run_suf, 0.0)
        run_pre = run_pre * jnp.where(after, 1.0, decays[c])
        run_suf = run_suf * jnp.where(after, decays[c], 1.0)
    pre = weighted_sum(w_pre, updates)
    suf = weighted_sum(w_suf, updates)
    gain_pre = run_pre
    gain_suf = run_suf
    gain_row = gain_pre * gain_suf
    row = pre + gain_pre * suf
    from_two_ahead = shift_x(pre, -1)
    through = shift_x(row + gain_row * from_two_ahead, -1)
    return suf + gain_suf * through


def per_device(queries, keys, values, grad_out, log_decay, doc_lengths):
    heads = lax.axis_size("head")
    rows = queries.shape[0]
    key_dim = queries.shape[1] // heads
    value_dim = values.shape[1] // heads
    packed = jnp.concatenate(
        [
            queries.reshape(rows, heads, key_dim),
            keys.reshape(rows, heads, key_dim),
            values.reshape(rows, heads, value_dim),
        ],
        axis=2,
    ).reshape(rows, heads * (2 * key_dim + value_dim))
    gathered = lax.all_to_all(packed, "head", split_axis=1, concat_axis=0, tiled=True)
    query_rows = gathered[:, :key_dim]
    key_rows = gathered[:, key_dim : 2 * key_dim]
    value_rows = gathered[:, 2 * key_dim :]
    tok_dev = key_rows.shape[0]
    block_count = tok_dev // BLOCK
    score_scaling = (key_dim * BLOCK) ** (-0.5)
    me = lax.axis_index("cx") * lax.axis_size("cy") + lax.axis_index("cy")
    doc_ids = document_ids(doc_lengths, me * tok_dev, tok_dev)
    weights, per_head_decay_rate, tail_decay, block_decay = decay_tables(
        log_decay[0], doc_ids, BLOCK, score_scaling
    )
    query_block_list = query_rows.reshape(block_count, BLOCK, key_dim)
    key_blocks = key_rows.reshape(block_count, BLOCK, key_dim)
    value_block_list = value_rows.reshape(block_count, BLOCK, value_dim)
    gradient_block_list = grad_out.reshape(block_count, BLOCK, value_dim)
    keyed_blocks = (key_blocks * tail_decay[:, :, None]).astype(jnp.bfloat16)
    queried = (query_block_list * (per_head_decay_rate * score_scaling)[:, :, None]).astype(
        jnp.bfloat16
    )
    forward_bundle = coded_bundle(keyed_blocks[0], value_block_list[0], block_decay[0])
    backward_bundle = coded_bundle(queried[0], gradient_block_list[0], block_decay[0])
    row_bundles = lax.all_gather(jnp.stack([forward_bundle, backward_bundle]), "cy")
    y = lax.axis_index("cy")
    forward_updates, row_decays = row_updates(row_bundles, 0, BLOCK, key_dim)
    backward_updates, _ = row_updates(row_bundles, 1, BLOCK, key_dim)
    states = forward_states(forward_updates, row_decays, y)[None]
    ends = backward_states(backward_updates, row_decays, y)[None]
    lowered_state = states.astype(jnp.bfloat16)
    back_low = ends.astype(jnp.bfloat16)
    scores = jnp.einsum(
        "nid,njd->nij", query_block_list, key_blocks, preferred_element_type=jnp.float32
    )
    attention_weights = (scores * weights).astype(jnp.bfloat16)
    retained = (
        jnp.einsum(
            "xho,xoy->xhy", query_block_list, lowered_state, preferred_element_type=jnp.float32
        )
        * (per_head_decay_rate * score_scaling)[:, :, None]
    )
    retained = retained + jnp.einsum(
        "bcv,bvd->bcd", attention_weights, value_block_list, preferred_element_type=jnp.float32
    )
    score_gradient = jnp.einsum(
        "ysb,ytb->yst", gradient_block_list, value_block_list, preferred_element_type=jnp.float32
    )
    gprobs = (score_gradient * weights).astype(jnp.bfloat16)
    query_gradient = (
        jnp.einsum(
            "srj,sqj->srq", gradient_block_list, lowered_state, preferred_element_type=jnp.float32
        )
        * (per_head_decay_rate * score_scaling)[:, :, None]
    )
    query_gradient = query_gradient + jnp.einsum(
        "nij,njd->nid", gprobs, key_blocks, preferred_element_type=jnp.float32
    )
    grad_k = (
        jnp.einsum("nje,nde->njd", value_block_list, back_low, preferred_element_type=jnp.float32)
        * tail_decay[:, :, None]
    )
    grad_k = grad_k + jnp.einsum(
        "nij,nid->njd", gprobs, query_block_list, preferred_element_type=jnp.float32
    )
    value_gradient = (
        jnp.einsum("njd,nde->nje", key_blocks, back_low, preferred_element_type=jnp.float32)
        * tail_decay[:, :, None]
    )
    value_gradient = value_gradient + jnp.einsum(
        "glu,glx->gux", attention_weights, gradient_block_list, preferred_element_type=jnp.float32
    )
    return (
        retained.reshape(tok_dev, value_dim).astype(jnp.bfloat16),
        query_gradient.reshape(tok_dev, key_dim).astype(jnp.bfloat16),
        grad_k.reshape(tok_dev, key_dim).astype(jnp.bfloat16),
        value_gradient.reshape(tok_dev, value_dim).astype(jnp.bfloat16),
    )


def solution(mesh):
    ctx_size = mesh.shape["ctx"]
    row_len = 8 if ctx_size % 8 == 0 else 1
    grid = Mesh(
        mesh.devices.reshape(ctx_size // row_len, row_len, mesh.shape["head"]),
        ("cx", "cy", "head"),
    )
    ctx = ("cx", "cy")
    placed = (
        P(ctx + ("head",), None),
        P(ctx + ("head",), None),
        P(ctx + ("head",), None),
        P(ctx, "head"),
        P("head", ctx),
        P(),
    )
    return jax.shard_map(
        per_device,
        mesh=grid,
        in_specs=placed,
        out_specs=(P(ctx, "head"), P(ctx, "head"), P(ctx, "head"), P(ctx, "head")),
        check_vma=False,
    )
```

```python
import jax
import jax.numpy as jnp
from jax import lax
from jax.sharding import PartitionSpec as P

BLOCK = 128
WINDOW_BLOCKS = 16


def passed_along(block, axis, distance):
    devices = range(lax.axis_size(axis))
    route = [(i - distance, i) for i in devices if i - distance in devices]
    return lax.ppermute(block, axis, route)


def document_ids(doc_lengths, first_place, span_length):
    starts = jnp.cumsum(doc_lengths, dtype=jnp.int32) - doc_lengths
    places = first_place - 1 + jnp.arange(span_length + 1, dtype=jnp.int32)
    return jnp.sum((starts[None, :] <= places[:, None]).astype(jnp.int32), axis=1) - 1


def decay_tables(log_rates, doc_ids, block_size, score_scaling):
    block_count = log_rates.shape[0] // block_size
    cumulated = jnp.cumsum(log_rates.reshape(block_count, block_size), axis=1)
    before = doc_ids[0 : block_count * block_size : block_size]
    own_ids = doc_ids[1:].reshape(block_count, block_size)
    carried = (own_ids == before[:, None]).astype(jnp.float32)
    last_ids = own_ids[:, block_size - 1]
    tail_mask = (own_ids == last_ids[:, None]).astype(jnp.float32)
    block_decay = jnp.exp(cumulated[:, block_size - 1]) * carried[:, block_size - 1]
    row_index = lax.broadcasted_iota(jnp.int32, (block_size, block_size), 0)
    column_index = lax.broadcasted_iota(jnp.int32, (block_size, block_size), 1)
    inside = (own_ids[:, :, None] == own_ids[:, None, :]) & (row_index >= column_index)[None]
    decay_gaps = cumulated[:, :, None] - cumulated[:, None, :]
    weights = jnp.where(inside, jnp.exp(jnp.where(inside, decay_gaps, 0.0)), 0.0) * score_scaling
    per_head_decay_rate = jnp.exp(cumulated) * carried
    tail_decay = jnp.exp(cumulated[:, block_size - 1 :] - cumulated) * tail_mask
    return (weights, per_head_decay_rate, tail_decay, block_decay)


RELAY_BLOCKS = WINDOW_BLOCKS // 2
GAIN_ROWS = 8
DIRECT_BLOCKS = 2


def pieces_of(decay):
    high = lax.reduce_precision(decay, exponent_bits=8, mantissa_bits=7)
    rest = decay - high
    middle = lax.reduce_precision(rest, exponent_bits=8, mantissa_bits=7)
    return jnp.stack([high, middle, rest - middle])


def relayed_partial(left, right, own_decay, direction):
    rows = left.shape[0]
    split = left.shape[1]
    cols = split + right.shape[1]
    parts = jnp.zeros((GAIN_ROWS, cols), jnp.float32).at[:3, :].set(pieces_of(own_decay)[:, None])
    moving = jnp.concatenate(
        [jnp.concatenate([left, right], axis=1), parts.astype(jnp.bfloat16)], axis=0
    )
    received = []
    own = moving
    for _ in range(RELAY_BLOCKS - DIRECT_BLOCKS):
        moving = passed_along(moving, "ctx", direction)
        received.append(moving)
    for k in range(RELAY_BLOCKS - DIRECT_BLOCKS + 1, RELAY_BLOCKS + 1):
        received.append(passed_along(own, "ctx", direction * k))
    stacked = jnp.stack(received)
    updates = jnp.einsum(
        "kcd,kce->kde",
        stacked[:, :rows, :split],
        stacked[:, :rows, split:],
        preferred_element_type=jnp.float32,
    )
    coded = stacked[:, rows : rows + 3, 0].astype(jnp.float32)
    decays = (coded[:, 0] + coded[:, 1]) + coded[:, 2]
    weights = [jnp.float32(1.0)]
    for k in range(1, RELAY_BLOCKS + 1):
        weights.append(weights[-1] * decays[k - 1])
    gain = weights[RELAY_BLOCKS]
    acc = updates[0]
    for k in range(1, RELAY_BLOCKS):
        acc = acc + weights[k] * updates[k]
    joined = passed_along(acc, "ctx", direction * RELAY_BLOCKS)
    return gain * joined + acc


def per_device(queries, keys, values, grad_out, log_decay, doc_lengths):
    heads = lax.axis_size("head")
    rows = queries.shape[0]
    key_dim = queries.shape[1] // heads
    value_dim = values.shape[1] // heads
    packed = jnp.concatenate(
        [
            queries.reshape(rows, heads, key_dim),
            keys.reshape(rows, heads, key_dim),
            values.reshape(rows, heads, value_dim),
        ],
        axis=2,
    ).reshape(rows, heads * (2 * key_dim + value_dim))
    gathered = lax.all_to_all(packed, "head", split_axis=1, concat_axis=0, tiled=True)
    query_rows = gathered[:, :key_dim]
    key_rows = gathered[:, key_dim : 2 * key_dim]
    value_rows = gathered[:, 2 * key_dim :]
    tok_dev = key_rows.shape[0]
    block_count = tok_dev // BLOCK
    score_scaling = (key_dim * BLOCK) ** (-0.5)
    me = lax.axis_index("ctx")
    doc_ids = document_ids(doc_lengths, me * tok_dev, tok_dev)
    weights, per_head_decay_rate, tail_decay, block_decay = decay_tables(
        log_decay[0], doc_ids, BLOCK, score_scaling
    )
    query_block_list = query_rows.reshape(block_count, BLOCK, key_dim)
    key_blocks = key_rows.reshape(block_count, BLOCK, key_dim)
    value_block_list = value_rows.reshape(block_count, BLOCK, value_dim)
    gradient_block_list = grad_out.reshape(block_count, BLOCK, value_dim)
    keyed_blocks = (key_blocks * tail_decay[:, :, None]).astype(jnp.bfloat16)
    queried = (query_block_list * (per_head_decay_rate * score_scaling)[:, :, None]).astype(
        jnp.bfloat16
    )
    states = relayed_partial(keyed_blocks[0], value_block_list[0], block_decay[0], 1)[None]
    ends = relayed_partial(queried[0], gradient_block_list[0], block_decay[0], -1)[None]
    lowered_state = states.astype(jnp.bfloat16)
    back_low = ends.astype(jnp.bfloat16)
    scores = jnp.einsum(
        "nid,njd->nij", query_block_list, key_blocks, preferred_element_type=jnp.float32
    )
    attention_weights = (scores * weights).astype(jnp.bfloat16)
    retained = (
        jnp.einsum(
            "xho,xoy->xhy", query_block_list, lowered_state, preferred_element_type=jnp.float32
        )
        * (per_head_decay_rate * score_scaling)[:, :, None]
    )
    retained = retained + jnp.einsum(
        "bcv,bvd->bcd", attention_weights, value_block_list, preferred_element_type=jnp.float32
    )
    score_gradient = jnp.einsum(
        "ysb,ytb->yst", gradient_block_list, value_block_list, preferred_element_type=jnp.float32
    )
    gprobs = (score_gradient * weights).astype(jnp.bfloat16)
    query_gradient = (
        jnp.einsum(
            "srj,sqj->srq", gradient_block_list, lowered_state, preferred_element_type=jnp.float32
        )
        * (per_head_decay_rate * score_scaling)[:, :, None]
    )
    query_gradient = query_gradient + jnp.einsum(
        "nij,njd->nid", gprobs, key_blocks, preferred_element_type=jnp.float32
    )
    grad_k = (
        jnp.einsum("nje,nde->njd", value_block_list, back_low, preferred_element_type=jnp.float32)
        * tail_decay[:, :, None]
    )
    grad_k = grad_k + jnp.einsum(
        "nij,nid->njd", gprobs, query_block_list, preferred_element_type=jnp.float32
    )
    value_gradient = (
        jnp.einsum("njd,nde->nje", key_blocks, back_low, preferred_element_type=jnp.float32)
        * tail_decay[:, :, None]
    )
    value_gradient = value_gradient + jnp.einsum(
        "glu,glx->gux", attention_weights, gradient_block_list, preferred_element_type=jnp.float32
    )
    return (
        retained.reshape(tok_dev, value_dim).astype(jnp.bfloat16),
        query_gradient.reshape(tok_dev, key_dim).astype(jnp.bfloat16),
        grad_k.reshape(tok_dev, key_dim).astype(jnp.bfloat16),
        value_gradient.reshape(tok_dev, value_dim).astype(jnp.bfloat16),
    )


def solution(mesh):
    placed = (
        P(("ctx", "head"), None),
        P(("ctx", "head"), None),
        P(("ctx", "head"), None),
        P("ctx", "head"),
        P("head", "ctx"),
        P(),
    )
    return jax.shard_map(
        per_device,
        mesh=mesh,
        in_specs=placed,
        out_specs=(P("ctx", "head"), P("ctx", "head"), P("ctx", "head"), P("ctx", "head")),
        check_vma=False,
    )
```

```python
import jax
import jax.numpy as jnp
from jax import lax
from jax.sharding import PartitionSpec as P

BLOCK = 128
WINDOW_BLOCKS = 16


def passed_along(block, axis, distance):
    devices = range(lax.axis_size(axis))
    route = [(i - distance, i) for i in devices if i - distance in devices]
    return lax.ppermute(block, axis, route)


def document_ids(doc_lengths, first_place, span_length):
    starts = jnp.cumsum(doc_lengths, dtype=jnp.int32) - doc_lengths
    places = first_place - 1 + jnp.arange(span_length + 1, dtype=jnp.int32)
    return jnp.sum((starts[None, :] <= places[:, None]).astype(jnp.int32), axis=1) - 1


def decay_tables(log_rates, doc_ids, block_size, score_scaling):
    block_count = log_rates.shape[0] // block_size
    cumulated = jnp.cumsum(log_rates.reshape(block_count, block_size), axis=1)
    before = doc_ids[0 : block_count * block_size : block_size]
    own_ids = doc_ids[1:].reshape(block_count, block_size)
    carried = (own_ids == before[:, None]).astype(jnp.float32)
    last_ids = own_ids[:, block_size - 1]
    tail_mask = (own_ids == last_ids[:, None]).astype(jnp.float32)
    block_decay = jnp.exp(cumulated[:, block_size - 1]) * carried[:, block_size - 1]
    row_index = lax.broadcasted_iota(jnp.int32, (block_size, block_size), 0)
    column_index = lax.broadcasted_iota(jnp.int32, (block_size, block_size), 1)
    inside = (own_ids[:, :, None] == own_ids[:, None, :]) & (row_index >= column_index)[None]
    decay_gaps = cumulated[:, :, None] - cumulated[:, None, :]
    weights = jnp.where(inside, jnp.exp(jnp.where(inside, decay_gaps, 0.0)), 0.0) * score_scaling
    per_head_decay_rate = jnp.exp(cumulated) * carried
    tail_decay = jnp.exp(cumulated[:, block_size - 1 :] - cumulated) * tail_mask
    return (weights, per_head_decay_rate, tail_decay, block_decay)


RELAY_BLOCKS = WINDOW_BLOCKS // 2
GAIN_ROWS = 8
DIRECT_BLOCKS = 2


def pieces_of(decay):
    high = lax.reduce_precision(decay, exponent_bits=8, mantissa_bits=7)
    rest = decay - high
    middle = lax.reduce_precision(rest, exponent_bits=8, mantissa_bits=7)
    return jnp.stack([high, middle, rest - middle])


def relayed_partial(left, right, own_decay, direction):
    rows = left.shape[0]
    split = left.shape[1]
    cols = split + right.shape[1]
    parts = jnp.zeros((GAIN_ROWS, cols), jnp.float32).at[:3, :].set(pieces_of(own_decay)[:, None])
    moving = jnp.concatenate(
        [jnp.concatenate([left, right], axis=1), parts.astype(jnp.bfloat16)], axis=0
    )
    received = []
    own = moving
    for _ in range(RELAY_BLOCKS - DIRECT_BLOCKS):
        moving = passed_along(moving, "ctx", direction)
        received.append(moving)
    for k in range(RELAY_BLOCKS - DIRECT_BLOCKS + 1, RELAY_BLOCKS + 1):
        received.append(passed_along(own, "ctx", direction * k))
    stacked = jnp.stack(received)
    updates = jnp.einsum(
        "kcd,kce->kde",
        stacked[:, :rows, :split],
        stacked[:, :rows, split:],
        preferred_element_type=jnp.float32,
    )
    coded = stacked[:, rows : rows + 3, 0].astype(jnp.float32)
    decays = (coded[:, 0] + coded[:, 1]) + coded[:, 2]
    weights = jnp.cumprod(jnp.concatenate([jnp.ones((1,), jnp.float32), decays]))
    gain = weights[RELAY_BLOCKS]
    acc = jnp.sum(weights[:RELAY_BLOCKS, None, None] * updates, axis=0)
    joined = passed_along(acc, "ctx", direction * RELAY_BLOCKS)
    return gain * joined + acc


def per_device(queries, keys, values, grad_out, log_decay, doc_lengths):
    heads = lax.axis_size("head")
    rows = queries.shape[0]
    key_dim = queries.shape[1] // heads
    value_dim = values.shape[1] // heads
    packed = jnp.concatenate(
        [
            queries.reshape(rows, heads, key_dim),
            keys.reshape(rows, heads, key_dim),
            values.reshape(rows, heads, value_dim),
        ],
        axis=2,
    ).reshape(rows, heads * (2 * key_dim + value_dim))
    gathered = lax.all_to_all(packed, "head", split_axis=1, concat_axis=0, tiled=True)
    query_rows = gathered[:, :key_dim]
    key_rows = gathered[:, key_dim : 2 * key_dim]
    value_rows = gathered[:, 2 * key_dim :]
    tok_dev = key_rows.shape[0]
    block_count = tok_dev // BLOCK
    score_scaling = (key_dim * BLOCK) ** (-0.5)
    me = lax.axis_index("ctx")
    doc_ids = document_ids(doc_lengths, me * tok_dev, tok_dev)
    weights, per_head_decay_rate, tail_decay, block_decay = decay_tables(
        log_decay[0], doc_ids, BLOCK, score_scaling
    )
    query_block_list = query_rows.reshape(block_count, BLOCK, key_dim)
    key_blocks = key_rows.reshape(block_count, BLOCK, key_dim)
    value_block_list = value_rows.reshape(block_count, BLOCK, value_dim)
    gradient_block_list = grad_out.reshape(block_count, BLOCK, value_dim)
    keyed_blocks = (key_blocks * tail_decay[:, :, None]).astype(jnp.bfloat16)
    queried = (query_block_list * (per_head_decay_rate * score_scaling)[:, :, None]).astype(
        jnp.bfloat16
    )
    states = relayed_partial(keyed_blocks[0], value_block_list[0], block_decay[0], 1)[None]
    ends = relayed_partial(queried[0], gradient_block_list[0], block_decay[0], -1)[None]
    lowered_state = states.astype(jnp.bfloat16)
    back_low = ends.astype(jnp.bfloat16)
    scores = jnp.einsum(
        "nid,njd->nij", query_block_list, key_blocks, preferred_element_type=jnp.float32
    )
    attention_weights = (scores * weights).astype(jnp.bfloat16)
    retained = (
        jnp.einsum(
            "xho,xoy->xhy", query_block_list, lowered_state, preferred_element_type=jnp.float32
        )
        * (per_head_decay_rate * score_scaling)[:, :, None]
    )
    retained = retained + jnp.einsum(
        "bcv,bvd->bcd", attention_weights, value_block_list, preferred_element_type=jnp.float32
    )
    score_gradient = jnp.einsum(
        "ysb,ytb->yst", gradient_block_list, value_block_list, preferred_element_type=jnp.float32
    )
    gprobs = (score_gradient * weights).astype(jnp.bfloat16)
    query_gradient = (
        jnp.einsum(
            "srj,sqj->srq", gradient_block_list, lowered_state, preferred_element_type=jnp.float32
        )
        * (per_head_decay_rate * score_scaling)[:, :, None]
    )
    query_gradient = query_gradient + jnp.einsum(
        "nij,njd->nid", gprobs, key_blocks, preferred_element_type=jnp.float32
    )
    grad_k = (
        jnp.einsum("nje,nde->njd", value_block_list, back_low, preferred_element_type=jnp.float32)
        * tail_decay[:, :, None]
    )
    grad_k = grad_k + jnp.einsum(
        "nij,nid->njd", gprobs, query_block_list, preferred_element_type=jnp.float32
    )
    value_gradient = (
        jnp.einsum("njd,nde->nje", key_blocks, back_low, preferred_element_type=jnp.float32)
        * tail_decay[:, :, None]
    )
    value_gradient = value_gradient + jnp.einsum(
        "glu,glx->gux", attention_weights, gradient_block_list, preferred_element_type=jnp.float32
    )
    return (
        retained.reshape(tok_dev, value_dim).astype(jnp.bfloat16),
        query_gradient.reshape(tok_dev, key_dim).astype(jnp.bfloat16),
        grad_k.reshape(tok_dev, key_dim).astype(jnp.bfloat16),
        value_gradient.reshape(tok_dev, value_dim).astype(jnp.bfloat16),
    )


def solution(mesh):
    placed = (
        P(("ctx", "head"), None),
        P(("ctx", "head"), None),
        P(("ctx", "head"), None),
        P("ctx", "head"),
        P("head", "ctx"),
        P(),
    )
    return jax.shard_map(
        per_device,
        mesh=mesh,
        in_specs=placed,
        out_specs=(P("ctx", "head"), P("ctx", "head"), P("ctx", "head"), P("ctx", "head")),
        check_vma=False,
    )
```

```python
import jax
import jax.numpy as jnp
from jax import lax
from jax.sharding import PartitionSpec as P

BLOCK = 128
WINDOW_BLOCKS = 16


def passed_along(block, axis, distance):
    devices = range(lax.axis_size(axis))
    route = [(i - distance, i) for i in devices if i - distance in devices]
    return lax.ppermute(block, axis, route)


def document_ids(doc_lengths, first_place, span_length):
    starts = jnp.cumsum(doc_lengths, dtype=jnp.int32) - doc_lengths
    places = first_place - 1 + jnp.arange(span_length + 1, dtype=jnp.int32)
    return jnp.sum((starts[None, :] <= places[:, None]).astype(jnp.int32), axis=1) - 1


def decay_tables(log_rates, doc_ids, block_size, score_scaling):
    block_count = log_rates.shape[0] // block_size
    cumulated = jnp.cumsum(log_rates.reshape(block_count, block_size), axis=1)
    before = doc_ids[0 : block_count * block_size : block_size]
    own_ids = doc_ids[1:].reshape(block_count, block_size)
    carried = (own_ids == before[:, None]).astype(jnp.float32)
    last_ids = own_ids[:, block_size - 1]
    tail_mask = (own_ids == last_ids[:, None]).astype(jnp.float32)
    block_decay = jnp.exp(cumulated[:, block_size - 1]) * carried[:, block_size - 1]
    row_index = lax.broadcasted_iota(jnp.int32, (block_size, block_size), 0)
    column_index = lax.broadcasted_iota(jnp.int32, (block_size, block_size), 1)
    inside = (own_ids[:, :, None] == own_ids[:, None, :]) & (row_index >= column_index)[None]
    decay_gaps = cumulated[:, :, None] - cumulated[:, None, :]
    weights = jnp.where(inside, jnp.exp(jnp.where(inside, decay_gaps, 0.0)), 0.0) * score_scaling
    per_head_decay_rate = jnp.exp(cumulated) * carried
    tail_decay = jnp.exp(cumulated[:, block_size - 1 :] - cumulated) * tail_mask
    return (weights, per_head_decay_rate, tail_decay, block_decay)


RELAY_BLOCKS = WINDOW_BLOCKS // 2
GAIN_ROWS = 8
DIRECT_BLOCKS = 3


def pieces_of(decay):
    high = lax.reduce_precision(decay, exponent_bits=8, mantissa_bits=7)
    rest = decay - high
    middle = lax.reduce_precision(rest, exponent_bits=8, mantissa_bits=7)
    return jnp.stack([high, middle, rest - middle])


def relayed_partial(left, right, own_decay, direction):
    rows = left.shape[0]
    split = left.shape[1]
    cols = split + right.shape[1]
    parts = jnp.zeros((GAIN_ROWS, cols), jnp.float32).at[:3, :].set(pieces_of(own_decay)[:, None])
    moving = jnp.concatenate(
        [jnp.concatenate([left, right], axis=1), parts.astype(jnp.bfloat16)], axis=0
    )
    received = []
    own = moving
    for _ in range(RELAY_BLOCKS - DIRECT_BLOCKS):
        moving = passed_along(moving, "ctx", direction)
        received.append(moving)
    for k in range(RELAY_BLOCKS - DIRECT_BLOCKS + 1, RELAY_BLOCKS + 1):
        received.append(passed_along(own, "ctx", direction * k))
    stacked = jnp.stack(received)
    updates = jnp.einsum(
        "kcd,kce->kde",
        stacked[:, :rows, :split],
        stacked[:, :rows, split:],
        preferred_element_type=jnp.float32,
    )
    coded = stacked[:, rows : rows + 3, 0].astype(jnp.float32)
    decays = (coded[:, 0] + coded[:, 1]) + coded[:, 2]
    weights = jnp.cumprod(jnp.concatenate([jnp.ones((1,), jnp.float32), decays]))
    gain = weights[RELAY_BLOCKS]
    acc = jnp.sum(weights[:RELAY_BLOCKS, None, None] * updates, axis=0)
    joined = passed_along(acc, "ctx", direction * RELAY_BLOCKS)
    return gain * joined + acc


def per_device(queries, keys, values, grad_out, log_decay, doc_lengths):
    heads = lax.axis_size("head")
    rows = queries.shape[0]
    key_dim = queries.shape[1] // heads
    value_dim = values.shape[1] // heads
    packed = jnp.concatenate(
        [
            queries.reshape(rows, heads, key_dim),
            keys.reshape(rows, heads, key_dim),
            values.reshape(rows, heads, value_dim),
        ],
        axis=2,
    ).reshape(rows, heads * (2 * key_dim + value_dim))
    gathered = lax.all_to_all(packed, "head", split_axis=1, concat_axis=0, tiled=True)
    query_rows = gathered[:, :key_dim]
    key_rows = gathered[:, key_dim : 2 * key_dim]
    value_rows = gathered[:, 2 * key_dim :]
    tok_dev = key_rows.shape[0]
    block_count = tok_dev // BLOCK
    score_scaling = (key_dim * BLOCK) ** (-0.5)
    me = lax.axis_index("ctx")
    doc_ids = document_ids(doc_lengths, me * tok_dev, tok_dev)
    weights, per_head_decay_rate, tail_decay, block_decay = decay_tables(
        log_decay[0], doc_ids, BLOCK, score_scaling
    )
    query_block_list = query_rows.reshape(block_count, BLOCK, key_dim)
    key_blocks = key_rows.reshape(block_count, BLOCK, key_dim)
    value_block_list = value_rows.reshape(block_count, BLOCK, value_dim)
    gradient_block_list = grad_out.reshape(block_count, BLOCK, value_dim)
    keyed_blocks = (key_blocks * tail_decay[:, :, None]).astype(jnp.bfloat16)
    queried = (query_block_list * (per_head_decay_rate * score_scaling)[:, :, None]).astype(
        jnp.bfloat16
    )
    states = relayed_partial(keyed_blocks[0], value_block_list[0], block_decay[0], 1)[None]
    ends = relayed_partial(queried[0], gradient_block_list[0], block_decay[0], -1)[None]
    lowered_state = states.astype(jnp.bfloat16)
    back_low = ends.astype(jnp.bfloat16)
    scores = jnp.einsum(
        "nid,njd->nij", query_block_list, key_blocks, preferred_element_type=jnp.float32
    )
    attention_weights = (scores * weights).astype(jnp.bfloat16)
    retained = (
        jnp.einsum(
            "xho,xoy->xhy", query_block_list, lowered_state, preferred_element_type=jnp.float32
        )
        * (per_head_decay_rate * score_scaling)[:, :, None]
    )
    retained = retained + jnp.einsum(
        "bcv,bvd->bcd", attention_weights, value_block_list, preferred_element_type=jnp.float32
    )
    score_gradient = jnp.einsum(
        "ysb,ytb->yst", gradient_block_list, value_block_list, preferred_element_type=jnp.float32
    )
    gprobs = (score_gradient * weights).astype(jnp.bfloat16)
    query_gradient = (
        jnp.einsum(
            "srj,sqj->srq", gradient_block_list, lowered_state, preferred_element_type=jnp.float32
        )
        * (per_head_decay_rate * score_scaling)[:, :, None]
    )
    query_gradient = query_gradient + jnp.einsum(
        "nij,njd->nid", gprobs, key_blocks, preferred_element_type=jnp.float32
    )
    grad_k = (
        jnp.einsum("nje,nde->njd", value_block_list, back_low, preferred_element_type=jnp.float32)
        * tail_decay[:, :, None]
    )
    grad_k = grad_k + jnp.einsum(
        "nij,nid->njd", gprobs, query_block_list, preferred_element_type=jnp.float32
    )
    value_gradient = (
        jnp.einsum("njd,nde->nje", key_blocks, back_low, preferred_element_type=jnp.float32)
        * tail_decay[:, :, None]
    )
    value_gradient = value_gradient + jnp.einsum(
        "glu,glx->gux", attention_weights, gradient_block_list, preferred_element_type=jnp.float32
    )
    return (
        retained.reshape(tok_dev, value_dim).astype(jnp.bfloat16),
        query_gradient.reshape(tok_dev, key_dim).astype(jnp.bfloat16),
        grad_k.reshape(tok_dev, key_dim).astype(jnp.bfloat16),
        value_gradient.reshape(tok_dev, value_dim).astype(jnp.bfloat16),
    )


def solution(mesh):
    placed = (
        P(("ctx", "head"), None),
        P(("ctx", "head"), None),
        P(("ctx", "head"), None),
        P("ctx", "head"),
        P("head", "ctx"),
        P(),
    )
    return jax.shard_map(
        per_device,
        mesh=mesh,
        in_specs=placed,
        out_specs=(P("ctx", "head"), P("ctx", "head"), P("ctx", "head"), P("ctx", "head")),
        check_vma=False,
    )
```

```python
import jax
import jax.numpy as jnp
from jax import lax
from jax.sharding import PartitionSpec as P

BLOCK = 128
WINDOW_BLOCKS = 16


def passed_along(block, axis, distance):
    devices = range(lax.axis_size(axis))
    route = [(i - distance, i) for i in devices if i - distance in devices]
    return lax.ppermute(block, axis, route)


def document_ids(doc_lengths, first_place, span_length):
    starts = jnp.cumsum(doc_lengths, dtype=jnp.int32) - doc_lengths
    places = first_place - 1 + jnp.arange(span_length + 1, dtype=jnp.int32)
    return jnp.sum((starts[None, :] <= places[:, None]).astype(jnp.int32), axis=1) - 1


def decay_tables(log_rates, doc_ids, block_size, score_scaling):
    block_count = log_rates.shape[0] // block_size
    cumulated = jnp.cumsum(log_rates.reshape(block_count, block_size), axis=1)
    before = doc_ids[0 : block_count * block_size : block_size]
    own_ids = doc_ids[1:].reshape(block_count, block_size)
    carried = (own_ids == before[:, None]).astype(jnp.float32)
    last_ids = own_ids[:, block_size - 1]
    tail_mask = (own_ids == last_ids[:, None]).astype(jnp.float32)
    block_decay = jnp.exp(cumulated[:, block_size - 1]) * carried[:, block_size - 1]
    row_index = lax.broadcasted_iota(jnp.int32, (block_size, block_size), 0)
    column_index = lax.broadcasted_iota(jnp.int32, (block_size, block_size), 1)
    inside = (own_ids[:, :, None] == own_ids[:, None, :]) & (row_index >= column_index)[None]
    decay_gaps = cumulated[:, :, None] - cumulated[:, None, :]
    weights = jnp.where(inside, jnp.exp(jnp.where(inside, decay_gaps, 0.0)), 0.0) * score_scaling
    per_head_decay_rate = jnp.exp(cumulated) * carried
    tail_decay = jnp.exp(cumulated[:, block_size - 1 :] - cumulated) * tail_mask
    return (weights, per_head_decay_rate, tail_decay, block_decay)


RELAY_BLOCKS = WINDOW_BLOCKS // 2
GAIN_ROWS = 8
DIRECT_BLOCKS = 8


def pieces_of(decay):
    high = lax.reduce_precision(decay, exponent_bits=8, mantissa_bits=7)
    rest = decay - high
    middle = lax.reduce_precision(rest, exponent_bits=8, mantissa_bits=7)
    return jnp.stack([high, middle, rest - middle])


def relayed_partial(left, right, own_decay, direction):
    rows = left.shape[0]
    split = left.shape[1]
    cols = split + right.shape[1]
    parts = jnp.zeros((GAIN_ROWS, cols), jnp.float32).at[:3, :].set(pieces_of(own_decay)[:, None])
    moving = jnp.concatenate(
        [jnp.concatenate([left, right], axis=1), parts.astype(jnp.bfloat16)], axis=0
    )
    received = []
    own = moving
    for _ in range(RELAY_BLOCKS - DIRECT_BLOCKS):
        moving = passed_along(moving, "ctx", direction)
        received.append(moving)
    for k in range(RELAY_BLOCKS - DIRECT_BLOCKS + 1, RELAY_BLOCKS + 1):
        received.append(passed_along(own, "ctx", direction * k))
    stacked = jnp.stack(received)
    updates = jnp.einsum(
        "kcd,kce->kde",
        stacked[:, :rows, :split],
        stacked[:, :rows, split:],
        preferred_element_type=jnp.float32,
    )
    coded = stacked[:, rows : rows + 3, 0].astype(jnp.float32)
    decays = (coded[:, 0] + coded[:, 1]) + coded[:, 2]
    weights = jnp.cumprod(jnp.concatenate([jnp.ones((1,), jnp.float32), decays]))
    gain = weights[RELAY_BLOCKS]
    acc = jnp.sum(weights[:RELAY_BLOCKS, None, None] * updates, axis=0)
    joined = passed_along(acc, "ctx", direction * RELAY_BLOCKS)
    return gain * joined + acc


def per_device(queries, keys, values, grad_out, log_decay, doc_lengths):
    heads = lax.axis_size("head")
    rows = queries.shape[0]
    key_dim = queries.shape[1] // heads
    value_dim = values.shape[1] // heads
    packed = jnp.concatenate(
        [
            queries.reshape(rows, heads, key_dim),
            keys.reshape(rows, heads, key_dim),
            values.reshape(rows, heads, value_dim),
        ],
        axis=2,
    ).reshape(rows, heads * (2 * key_dim + value_dim))
    gathered = lax.all_to_all(packed, "head", split_axis=1, concat_axis=0, tiled=True)
    query_rows = gathered[:, :key_dim]
    key_rows = gathered[:, key_dim : 2 * key_dim]
    value_rows = gathered[:, 2 * key_dim :]
    tok_dev = key_rows.shape[0]
    block_count = tok_dev // BLOCK
    score_scaling = (key_dim * BLOCK) ** (-0.5)
    me = lax.axis_index("ctx")
    doc_ids = document_ids(doc_lengths, me * tok_dev, tok_dev)
    weights, per_head_decay_rate, tail_decay, block_decay = decay_tables(
        log_decay[0], doc_ids, BLOCK, score_scaling
    )
    query_block_list = query_rows.reshape(block_count, BLOCK, key_dim)
    key_blocks = key_rows.reshape(block_count, BLOCK, key_dim)
    value_block_list = value_rows.reshape(block_count, BLOCK, value_dim)
    gradient_block_list = grad_out.reshape(block_count, BLOCK, value_dim)
    keyed_blocks = (key_blocks * tail_decay[:, :, None]).astype(jnp.bfloat16)
    queried = (query_block_list * (per_head_decay_rate * score_scaling)[:, :, None]).astype(
        jnp.bfloat16
    )
    states = relayed_partial(keyed_blocks[0], value_block_list[0], block_decay[0], 1)[None]
    ends = relayed_partial(queried[0], gradient_block_list[0], block_decay[0], -1)[None]
    lowered_state = states.astype(jnp.bfloat16)
    back_low = ends.astype(jnp.bfloat16)
    scores = jnp.einsum(
        "nid,njd->nij", query_block_list, key_blocks, preferred_element_type=jnp.float32
    )
    attention_weights = (scores * weights).astype(jnp.bfloat16)
    retained = (
        jnp.einsum(
            "xho,xoy->xhy", query_block_list, lowered_state, preferred_element_type=jnp.float32
        )
        * (per_head_decay_rate * score_scaling)[:, :, None]
    )
    retained = retained + jnp.einsum(
        "bcv,bvd->bcd", attention_weights, value_block_list, preferred_element_type=jnp.float32
    )
    score_gradient = jnp.einsum(
        "ysb,ytb->yst", gradient_block_list, value_block_list, preferred_element_type=jnp.float32
    )
    gprobs = (score_gradient * weights).astype(jnp.bfloat16)
    query_gradient = (
        jnp.einsum(
            "srj,sqj->srq", gradient_block_list, lowered_state, preferred_element_type=jnp.float32
        )
        * (per_head_decay_rate * score_scaling)[:, :, None]
    )
    query_gradient = query_gradient + jnp.einsum(
        "nij,njd->nid", gprobs, key_blocks, preferred_element_type=jnp.float32
    )
    grad_k = (
        jnp.einsum("nje,nde->njd", value_block_list, back_low, preferred_element_type=jnp.float32)
        * tail_decay[:, :, None]
    )
    grad_k = grad_k + jnp.einsum(
        "nij,nid->njd", gprobs, query_block_list, preferred_element_type=jnp.float32
    )
    value_gradient = (
        jnp.einsum("njd,nde->nje", key_blocks, back_low, preferred_element_type=jnp.float32)
        * tail_decay[:, :, None]
    )
    value_gradient = value_gradient + jnp.einsum(
        "glu,glx->gux", attention_weights, gradient_block_list, preferred_element_type=jnp.float32
    )
    return (
        retained.reshape(tok_dev, value_dim).astype(jnp.bfloat16),
        query_gradient.reshape(tok_dev, key_dim).astype(jnp.bfloat16),
        grad_k.reshape(tok_dev, key_dim).astype(jnp.bfloat16),
        value_gradient.reshape(tok_dev, value_dim).astype(jnp.bfloat16),
    )


def solution(mesh):
    placed = (
        P(("ctx", "head"), None),
        P(("ctx", "head"), None),
        P(("ctx", "head"), None),
        P("ctx", "head"),
        P("head", "ctx"),
        P(),
    )
    return jax.shard_map(
        per_device,
        mesh=mesh,
        in_specs=placed,
        out_specs=(P("ctx", "head"), P("ctx", "head"), P("ctx", "head"), P("ctx", "head")),
        check_vma=False,
    )
```

```python
import jax
import jax.numpy as jnp
from jax import lax
from jax.sharding import PartitionSpec as P

BLOCK = 128
WINDOW_BLOCKS = 16


def passed_along(block, axis, distance):
    devices = range(lax.axis_size(axis))
    route = [(i - distance, i) for i in devices if i - distance in devices]
    return lax.ppermute(block, axis, route)


def document_ids(doc_lengths, first_place, span_length):
    starts = jnp.cumsum(doc_lengths, dtype=jnp.int32) - doc_lengths
    places = first_place - 1 + jnp.arange(span_length + 1, dtype=jnp.int32)
    return jnp.sum((starts[None, :] <= places[:, None]).astype(jnp.int32), axis=1) - 1


def decay_tables(log_rates, doc_ids, block_size, score_scaling):
    block_count = log_rates.shape[0] // block_size
    cumulated = jnp.cumsum(log_rates.reshape(block_count, block_size), axis=1)
    before = doc_ids[0 : block_count * block_size : block_size]
    own_ids = doc_ids[1:].reshape(block_count, block_size)
    carried = (own_ids == before[:, None]).astype(jnp.float32)
    last_ids = own_ids[:, block_size - 1]
    tail_mask = (own_ids == last_ids[:, None]).astype(jnp.float32)
    block_decay = jnp.exp(cumulated[:, block_size - 1]) * carried[:, block_size - 1]
    row_index = lax.broadcasted_iota(jnp.int32, (block_size, block_size), 0)
    column_index = lax.broadcasted_iota(jnp.int32, (block_size, block_size), 1)
    inside = (own_ids[:, :, None] == own_ids[:, None, :]) & (row_index >= column_index)[None]
    decay_gaps = cumulated[:, :, None] - cumulated[:, None, :]
    weights = jnp.where(inside, jnp.exp(jnp.where(inside, decay_gaps, 0.0)), 0.0) * score_scaling
    per_head_decay_rate = jnp.exp(cumulated) * carried
    tail_decay = jnp.exp(cumulated[:, block_size - 1 :] - cumulated) * tail_mask
    return (weights, per_head_decay_rate, tail_decay, block_decay)


RELAY_BLOCKS = WINDOW_BLOCKS // 2
GAIN_ROWS = 8
DIRECT_BLOCKS = 4


def pieces_of(decay):
    high = lax.reduce_precision(decay, exponent_bits=8, mantissa_bits=7)
    rest = decay - high
    middle = lax.reduce_precision(rest, exponent_bits=8, mantissa_bits=7)
    return jnp.stack([high, middle, rest - middle])


def relayed_partial(left, right, own_decay, direction):
    rows = left.shape[0]
    split = left.shape[1]
    cols = split + right.shape[1]
    parts = jnp.zeros((GAIN_ROWS, cols), jnp.float32).at[:3, :].set(pieces_of(own_decay)[:, None])
    moving = jnp.concatenate(
        [jnp.concatenate([left, right], axis=1), parts.astype(jnp.bfloat16)], axis=0
    )
    received = []
    own = moving
    for _ in range(RELAY_BLOCKS - DIRECT_BLOCKS):
        moving = passed_along(moving, "ctx", direction)
        received.append(moving)
    for k in range(RELAY_BLOCKS - DIRECT_BLOCKS + 1, RELAY_BLOCKS + 1):
        received.append(passed_along(own, "ctx", direction * k))
    stacked = jnp.stack(received)
    updates = jnp.einsum(
        "kcd,kce->kde",
        stacked[:, :rows, :split],
        stacked[:, :rows, split:],
        preferred_element_type=jnp.float32,
    )
    coded = stacked[:, rows : rows + 3, 0].astype(jnp.float32)
    decays = (coded[:, 0] + coded[:, 1]) + coded[:, 2]
    weights = jnp.cumprod(jnp.concatenate([jnp.ones((1,), jnp.float32), decays]))
    gain = weights[RELAY_BLOCKS]
    acc = jnp.sum(weights[:RELAY_BLOCKS, None, None] * updates, axis=0)
    joined = passed_along(acc, "ctx", direction * RELAY_BLOCKS)
    return gain * joined + acc


def per_device(queries, keys, values, grad_out, log_decay, doc_lengths):
    heads = lax.axis_size("head")
    rows = queries.shape[0]
    key_dim = queries.shape[1] // heads
    value_dim = values.shape[1] // heads
    packed = jnp.concatenate(
        [
            queries.reshape(rows, heads, key_dim),
            keys.reshape(rows, heads, key_dim),
            values.reshape(rows, heads, value_dim),
        ],
        axis=2,
    ).reshape(rows, heads * (2 * key_dim + value_dim))
    gathered = lax.all_to_all(packed, "head", split_axis=1, concat_axis=0, tiled=True)
    query_rows = gathered[:, :key_dim]
    key_rows = gathered[:, key_dim : 2 * key_dim]
    value_rows = gathered[:, 2 * key_dim :]
    tok_dev = key_rows.shape[0]
    block_count = tok_dev // BLOCK
    score_scaling = (key_dim * BLOCK) ** (-0.5)
    me = lax.axis_index("ctx")
    doc_ids = document_ids(doc_lengths, me * tok_dev, tok_dev)
    weights, per_head_decay_rate, tail_decay, block_decay = decay_tables(
        log_decay[0], doc_ids, BLOCK, score_scaling
    )
    query_block_list = query_rows.reshape(block_count, BLOCK, key_dim)
    key_blocks = key_rows.reshape(block_count, BLOCK, key_dim)
    value_block_list = value_rows.reshape(block_count, BLOCK, value_dim)
    gradient_block_list = grad_out.reshape(block_count, BLOCK, value_dim)
    keyed_blocks = (key_blocks * tail_decay[:, :, None]).astype(jnp.bfloat16)
    queried = (query_block_list * (per_head_decay_rate * score_scaling)[:, :, None]).astype(
        jnp.bfloat16
    )
    states = relayed_partial(keyed_blocks[0], value_block_list[0], block_decay[0], 1)[None]
    ends = relayed_partial(queried[0], gradient_block_list[0], block_decay[0], -1)[None]
    lowered_state = states.astype(jnp.bfloat16)
    back_low = ends.astype(jnp.bfloat16)
    scores = jnp.einsum(
        "nid,njd->nij", query_block_list, key_blocks, preferred_element_type=jnp.float32
    )
    attention_weights = (scores * weights).astype(jnp.bfloat16)
    retained = (
        jnp.einsum(
            "xho,xoy->xhy", query_block_list, lowered_state, preferred_element_type=jnp.float32
        )
        * (per_head_decay_rate * score_scaling)[:, :, None]
    )
    retained = retained + jnp.einsum(
        "bcv,bvd->bcd", attention_weights, value_block_list, preferred_element_type=jnp.float32
    )
    score_gradient = jnp.einsum(
        "ysb,ytb->yst", gradient_block_list, value_block_list, preferred_element_type=jnp.float32
    )
    gprobs = (score_gradient * weights).astype(jnp.bfloat16)
    query_gradient = (
        jnp.einsum(
            "srj,sqj->srq", gradient_block_list, lowered_state, preferred_element_type=jnp.float32
        )
        * (per_head_decay_rate * score_scaling)[:, :, None]
    )
    query_gradient = query_gradient + jnp.einsum(
        "nij,njd->nid", gprobs, key_blocks, preferred_element_type=jnp.float32
    )
    grad_k = (
        jnp.einsum("nje,nde->njd", value_block_list, back_low, preferred_element_type=jnp.float32)
        * tail_decay[:, :, None]
    )
    grad_k = grad_k + jnp.einsum(
        "nij,nid->njd", gprobs, query_block_list, preferred_element_type=jnp.float32
    )
    value_gradient = (
        jnp.einsum("njd,nde->nje", key_blocks, back_low, preferred_element_type=jnp.float32)
        * tail_decay[:, :, None]
    )
    value_gradient = value_gradient + jnp.einsum(
        "glu,glx->gux", attention_weights, gradient_block_list, preferred_element_type=jnp.float32
    )
    return (
        retained.reshape(tok_dev, value_dim).astype(jnp.bfloat16),
        query_gradient.reshape(tok_dev, key_dim).astype(jnp.bfloat16),
        grad_k.reshape(tok_dev, key_dim).astype(jnp.bfloat16),
        value_gradient.reshape(tok_dev, value_dim).astype(jnp.bfloat16),
    )


def solution(mesh):
    placed = (
        P(("ctx", "head"), None),
        P(("ctx", "head"), None),
        P(("ctx", "head"), None),
        P("ctx", "head"),
        P("head", "ctx"),
        P(),
    )
    return jax.shard_map(
        per_device,
        mesh=mesh,
        in_specs=placed,
        out_specs=(P("ctx", "head"), P("ctx", "head"), P("ctx", "head"), P("ctx", "head")),
        check_vma=False,
    )
```
